32 devices in a mesh: seq: 4 (over y, x), exp: 8 (over z, core).
Axes of the slice: x: 2, y: 2, z: 4, core: 2. Of those that a mesh axis runs over, the one named last changes fastest.
Arguments:
- token_ids: int32 [4, 32], replicated, may hold values from 0 to 51199
- cache_lengths: int32 [32], replicated, may hold values from 1 to 1024, as said below
- empty_blocks: int32 [32, 64], replicated, may hold values 0 or 1
- expert_ids: int32 [4, 32, 6], replicated, may hold values from 0 to 63, all different within a row
- embed_table: bfloat16 [51200, 2048], P(('seq', 'exp')), may hold values from -3 to 3
- attn_gain: float32 [2048], replicated, may hold values from 0.5 to 1.5
- w_query: bfloat16 [2048, 2048], P(None, 'seq'), may hold values from -0.125 to 0.125
- w_key: bfloat16 [2048, 2048], P(None, 'seq'), may hold values from -0.125 to 0.125
- w_value: bfloat16 [2048, 2048], P(None, 'seq'), may hold values from -0.125 to 0.125
- w_out: bfloat16 [2048, 2048], P('seq'), may hold values from -0.125 to 0.125
- k_cache: bfloat16 [32, 1024, 2048], P('exp', 'seq'), may hold values from -200 to 200
- v_cache: bfloat16 [32, 1024, 2048], P('exp', 'seq'), may hold values from -6 to 6
- moe_gain: float32 [2048], replicated, may hold values from 0.5 to 1.5
- w_router: bfloat16 [2048, 64], replicated, may hold values from -0.125 to 0.125
- gate_pieces: bfloat16 [256, 2048, 352], P(('seq', 'exp')), may hold values from -0.125 to 0.125
- up_pieces: bfloat16 [256, 2048, 352], P(('seq', 'exp')), may hold values from -0.125 to 0.125
- down_pieces: bfloat16 [256, 352, 2048], P(('seq', 'exp')), may hold values from -0.15625 to 0.15625
- shared_gate: bfloat16 [2048, 2816], P(None, 'exp'), may hold values from -0.125 to 0.125
- shared_up: bfloat16 [2048, 2816], P(None, 'exp'), may hold values from -0.125 to 0.125
- shared_down: bfloat16 [2816, 2048], P('exp'), may hold values from -0.109375 to 0.109375
- final_gain: float32 [2048], replicated, may hold values from 0.5 to 1.5
- w_head: bfloat16 [2048, 51200], P(None, ('seq', 'exp')), may hold values from -0.125 to 0.125
Outputs:
- hidden_norms: float32 [4, 32], replicated
- greatest_logits: float32 [4, 32], replicated
The draws below stay inside these ranges and needn't reach their ends.
Inputs may be any that keep to these rules, and one draw needn't show every extreme that they name: `cache_lengths`: one of the 32 requests has exactly 1024 cached positions in every draw.
All inputs are finite; a program needn't handle non-finite values.
Results may differ from the reference program's by a relative error of at most 0.0055.
Values may be sent and summed in bfloat16 or wider, within the bound.
No kernel may reach another device: no remote copies, remote signals or barrier semaphores. Data moves between devices by JAX's collectives and lax.ppermute only.
A program may use at most 128 MiB of HBM per device.

```python
import math
import jax
import jax.numpy as jnp
import numpy as np
from jax import lax

D = 2048
HEADS = 16
HDIM = 128
EXPERTS = 64
TOPK = 6
FF = 1408
SFF = 2816
VOCAB = 51200
PIECES = 4
FFP = 352
BLK = 16
STEPS = 4
R = 32
LMAX = 1024
NBLK = 64


def draw_cache_lengths(key, part):
    length_key, longest_key = jax.random.split(key)
    lengths = jax.random.randint(length_key, (R,), 1, LMAX + 1)
    longest = jax.random.randint(longest_key, (), 0, R)
    return jnp.where(jnp.arange(R) == longest, LMAX, lengths).astype(jnp.int32)


def draw_k_cache(key, part):
    base_key = jax.random.fold_in(key, 0)
    cache_shape = (R, LMAX, HEADS * HDIM)
    base_values = 2.0 * jax.random.normal(base_key, cache_shape, jnp.float32)
    return jnp.clip(base_values, -16.0, 16.0).astype(jnp.bfloat16)


def plant(values, own_key, smallest, high):
    place = [jax.random.randint(jax.random.fold_in(own_key, axis), (), 0, length) for axis, length in enumerate(values.shape)]
    widest = values.shape.index(max(values.shape))
    neighbour = place[:widest] + [(place[widest] + 1) % values.shape[widest]] + place[widest + 1:]
    return values.at[tuple(place)].set(smallest).at[tuple(neighbour)].set(high)


def block_levels(key, shape, pieces, least, high):
    def one(position, parts):
        heights = jax.random.uniform(jax.random.fold_in(jax.random.fold_in(key, 6), position), (parts,), jnp.float32, least / len(pieces), high / len(pieces))
        return jnp.repeat(jnp.exp(heights), shape[position] // parts).reshape((-1,) + (1,) * (len(shape) - position - 1))

    factor_of = one(*pieces[0])
    for cut in pieces[1:]:
        factor_of = factor_of * one(*cut)
    return factor_of


def cumulative_ranks(number_of, lean):
    weights = [(1 << 20) // math.isqrt(standing ** lean) + 1 for standing in range(1, number_of + 1)]
    width = 1 + sum(weights) // (1 << 30)
    return np.cumsum(np.array([max(1, weight // width) for weight in weights]))


def ranked_ids(stream_key, extent, number_of, slope):
    grid = cumulative_ranks(number_of, slope)
    pick = jax.random.randint(jax.random.fold_in(stream_key, 1), extent, 0, int(grid[number_of - 1]))
    grade = jnp.searchsorted(jnp.asarray(grid, jnp.int32), pick, side="right")
    return jax.random.permutation(jax.random.fold_in(stream_key, 2), number_of)[grade].astype(jnp.int32)


def picks_of(rng, rows, amount, top, lift):
    sequence = jax.random.permutation(jax.random.fold_in(rng, 1), amount)
    favour = sequence
    for power in range(3):
        favour = favour * favour // amount
    favour = favour * lift // amount
    tickets = jax.random.randint(jax.random.fold_in(rng, 2), (rows, amount), 0, 4096) + favour
    holders = jax.random.permutation(jax.random.fold_in(rng, 3), rows)[jnp.arange(amount) % rows]
    tickets = jnp.where(jnp.arange(rows)[:, None] == holders[None, :], 1 << 14, tickets)
    merit = tickets * amount + jnp.arange(amount)
    return lax.top_k(merit.astype(jnp.int32), top)[1].astype(jnp.int32)


def centred(own_key, extent, scale, limit, cuts=(), kind=jnp.bfloat16):
    entries = scale * jax.random.normal(own_key, extent, jnp.float32)
    if cuts:
        entries = entries * block_levels(own_key, extent, cuts, -0.22, 0.18)
    return jnp.clip(entries, -limit, limit).astype(kind)


def setup_inputs(seed: int = 0) -> dict:
    keys = jax.random.split(jax.random.key(seed), 23)
    return {
        "token_ids": plant(ranked_ids(keys[0], (STEPS, R), VOCAB, 2), jax.random.fold_in(keys[0], 3), 0, VOCAB - 1).astype(jnp.int32),
        "cache_lengths": draw_cache_lengths(jax.random.fold_in(keys[22], 71), 0),
        "empty_blocks": plant((jax.random.randint(keys[2], (R, NBLK), 0, 4) < 1).astype(jnp.int32), jax.random.fold_in(keys[2], 1), 0, 1),
        "expert_ids": picks_of(keys[3], STEPS * R, EXPERTS, TOPK, 768).reshape((STEPS, R, TOPK)),
        "embed_table": centred(keys[4], (VOCAB, D), 0.5, 3.0, ((0, 32),)),
        "attn_gain": jnp.clip(1.0 + 0.1 * jax.random.normal(keys[5], (D,), jnp.float32), 0.5, 1.5),
        "w_query": centred(keys[6], (D, HEADS * HDIM), D ** -0.5, 0.125, ((1, 4),)),
        "w_key": centred(keys[7], (D, HEADS * HDIM), D ** -0.5, 0.125, ((1, 4),)),
        "w_value": centred(keys[8], (D, HEADS * HDIM), D ** -0.5, 0.125, ((1, 4),)),
        "w_out": centred(keys[9], (HEADS * HDIM, D), (HEADS * HDIM) ** -0.5, 0.125, ((0, 4),)),
        "k_cache": draw_k_cache(jax.random.fold_in(keys[22], 71), 0),
        "v_cache": centred(keys[11], (R, LMAX, HEADS * HDIM), 1.0, 6.0, ((0, 8), (1, 4))),
        "moe_gain": jnp.clip(1.0 + 0.1 * jax.random.normal(keys[12], (D,), jnp.float32), 0.5, 1.5),
        "w_router": centred(keys[13], (D, EXPERTS), D ** -0.5, 0.125),
        "gate_pieces": centred(keys[14], (EXPERTS * PIECES, D, FFP), D ** -0.5, 0.125, ((0, 32),)),
        "up_pieces": centred(keys[15], (EXPERTS * PIECES, D, FFP), D ** -0.5, 0.125, ((0, 32),)),
        "down_pieces": centred(keys[16], (EXPERTS * PIECES, FFP, D), FF ** -0.5, 0.15625, ((0, 32),)),
        "shared_gate": centred(keys[17], (D, SFF), D ** -0.5, 0.125, ((1, 8),)),
        "shared_up": centred(keys[18], (D, SFF), D ** -0.5, 0.125, ((1, 8),)),
        "shared_down": centred(keys[19], (SFF, D), SFF ** -0.5, 0.109375, ((0, 8),)),
        "final_gain": jnp.clip(1.0 + 0.1 * jax.random.normal(keys[20], (D,), jnp.float32), 0.5, 1.5),
        "w_head": centred(keys[21], (D, VOCAB), D ** -0.5, 0.125, ((1, 32),)),
    }


epsilon = 1e-06
negative = -1e+30

def rms_scale(values, scales):
    return values * lax.rsqrt(lax.optimization_barrier(jnp.mean(values * values, axis=-1, keepdims=True)) + epsilon) * scales

def rotate(values, places):
    half_width = values.shape[-1] // 2
    frequency = 10000.0 ** (-2.0 * jnp.arange(half_width, dtype=jnp.float32) / values.shape[-1])
    angles = places.astype(jnp.float32)[..., None, None] * frequency
    cosine_table = jnp.cos(angles)
    sine_table = jnp.sin(angles)
    lower = values[..., :half_width]
    upper = values[..., half_width:]
    return jnp.concatenate([lower * cosine_table - upper * sine_table, upper * cosine_table + lower * sine_table], axis=-1)

def widen(values):
    return lax.optimization_barrier(values.astype(jnp.bfloat16)).astype(jnp.float32)

def reference(token_ids, cache_lengths, empty_blocks, expert_ids, embed_table, attn_gain, w_query, w_key, w_value, w_out, k_cache, v_cache, moe_gain, w_router, gate_pieces, up_pieces, down_pieces, shared_gate, shared_up, shared_down, final_gain, w_head):
    tokens = STEPS * R
    embedded = embed_table[token_ids.reshape(tokens)].astype(jnp.float32)
    attn_in = rms_scale(embedded, attn_gain).astype(jnp.bfloat16)
    places = (cache_lengths[None, :] + jnp.arange(STEPS, dtype=jnp.int32)[:, None]).reshape(tokens)

    def project(weight):
        return jnp.dot(attn_in, weight, preferred_element_type=jnp.float32).reshape(tokens, HEADS, HDIM)
    queries = rotate(project(w_query), places).astype(jnp.bfloat16).reshape(STEPS, R, HEADS, HDIM)
    new_keys = rotate(project(w_key), places).astype(jnp.bfloat16).reshape(STEPS, R, HEADS, HDIM)
    new_values = project(w_value).astype(jnp.bfloat16).reshape(STEPS, R, HEADS, HDIM)
    positions = jnp.arange(LMAX, dtype=jnp.int32)
    blocked = jnp.broadcast_to(empty_blocks[:, :, None], (R, NBLK, BLK)).reshape(R, LMAX)
    live_mask = (positions[None, :] < cache_lengths[:, None]) & (blocked == 0)
    causal = jnp.arange(STEPS)[None, :] <= jnp.arange(STEPS)[:, None]
    score_scale = 1.0 / math.sqrt(HDIM)

    def one_head(head_index):
        start = (head_index * HDIM).astype(jnp.int32)
        query_head = lax.dynamic_index_in_dim(queries, head_index, 2, keepdims=False).astype(jnp.float32)
        key_head = lax.dynamic_slice_in_dim(k_cache, start, HDIM, 2).astype(jnp.float32)
        value_head = lax.dynamic_slice_in_dim(v_cache, start, HDIM, 2).astype(jnp.float32)
        fresh_keys = lax.dynamic_index_in_dim(new_keys, head_index, 2, keepdims=False).astype(jnp.float32)
        fresh_values = lax.dynamic_index_in_dim(new_values, head_index, 2, keepdims=False).astype(jnp.float32)
        cached = jnp.einsum('trd,rpd->trp', query_head, key_head) * score_scale
        fresh_scores = jnp.einsum('trd,urd->tru', query_head, fresh_keys) * score_scale
        cached_ok = live_mask[None, :, :]
        fresh_ok = causal[:, None, :]
        top_score = jnp.maximum(lax.optimization_barrier(jnp.max(jnp.where(cached_ok, cached, negative), axis=2)), lax.optimization_barrier(jnp.max(jnp.where(fresh_ok, fresh_scores, negative), axis=2)))
        cached_weights = jnp.where(cached_ok, jnp.exp(cached - top_score[..., None]), 0.0)
        fresh_weights = jnp.where(fresh_ok, jnp.exp(fresh_scores - top_score[..., None]), 0.0)
        totals = lax.optimization_barrier(jnp.sum(cached_weights, axis=2)) + lax.optimization_barrier(jnp.sum(fresh_weights, axis=2))
        mixture = jnp.einsum('trp,rpd->trd', widen(cached_weights), value_head) + jnp.einsum('tru,urd->trd', widen(fresh_weights), fresh_values)
        return (mixture / totals[..., None]).astype(jnp.bfloat16)
    heads_out = lax.map(one_head, jnp.arange(HEADS, dtype=jnp.int32))
    heads_out = jnp.transpose(heads_out, (1, 2, 0, 3)).reshape(tokens, HEADS * HDIM)
    resid = embedded + jnp.dot(heads_out, w_out, preferred_element_type=jnp.float32)
    moe_in = rms_scale(resid, moe_gain).astype(jnp.bfloat16)
    router = jax.nn.sigmoid(jnp.dot(moe_in, w_router, preferred_element_type=jnp.float32))
    chosen_ids = expert_ids.reshape(tokens, TOPK)
    chosen = jnp.take_along_axis(router, chosen_ids, axis=1)
    gate_weights = chosen / lax.optimization_barrier(jnp.sum(chosen, axis=1, keepdims=True))
    gate_full = gate_pieces.reshape(EXPERTS, PIECES, D, FFP)
    up_full = up_pieces.reshape(EXPERTS, PIECES, D, FFP)
    down_full = down_pieces.reshape(EXPERTS, PIECES, FFP, D)

    def one_token(token_item):
        token_row, id_row, weight_row = token_item
        row_wide = token_row.astype(jnp.float32)
        gate_rows = gate_full[id_row].astype(jnp.float32)
        up_rows = up_full[id_row].astype(jnp.float32)
        down_rows = down_full[id_row].astype(jnp.float32)
        hidden = jax.nn.silu(jnp.einsum('d,kpdf->kpf', row_wide, gate_rows)) * jnp.einsum('d,kpdf->kpf', row_wide, up_rows)
        outputs = jnp.einsum('kpf,kpfd->kd', widen(hidden), down_rows)
        return jnp.einsum('k,kd->d', weight_row, outputs)
    routed = lax.map(one_token, (moe_in, chosen_ids, gate_weights))
    shared_hidden = (jax.nn.silu(jnp.dot(moe_in, shared_gate, preferred_element_type=jnp.float32)) * jnp.dot(moe_in, shared_up, preferred_element_type=jnp.float32)).astype(jnp.bfloat16)
    final_hidden = resid + routed + jnp.dot(shared_hidden, shared_down, preferred_element_type=jnp.float32)
    hidden_norms = jnp.sqrt(lax.optimization_barrier(jnp.mean(final_hidden * final_hidden, axis=-1))).reshape(STEPS, R)
    head_in = rms_scale(final_hidden, final_gain).astype(jnp.bfloat16)
    logits = jnp.dot(head_in, w_head, preferred_element_type=jnp.float32)
    greatest_logits = lax.optimization_barrier(jnp.max(logits, axis=-1)).reshape(STEPS, R)
    return (hidden_norms, greatest_logits)
```

```python
import math

import jax
import jax.numpy as jnp
from jax import lax
from jax.sharding import PartitionSpec as P

HDIM = 128
PIECES = 4
BLK = 16


epsilon = 1e-06
negative = -1e30


def rms_scale(values, scales):
    return values * lax.rsqrt(jnp.mean(values * values, axis=-1, keepdims=True) + epsilon) * scales


def rotate(values, places):
    half_width = values.shape[-1] // 2
    frequency = 10000.0 ** (-2.0 * jnp.arange(half_width, dtype=jnp.float32) / values.shape[-1])
    angles = places.astype(jnp.float32)[..., None, None] * frequency
    cosine_table = jnp.cos(angles)
    sine_table = jnp.sin(angles)
    lower = values[..., :half_width]
    upper = values[..., half_width:]
    return jnp.concatenate(
        [lower * cosine_table - upper * sine_table, upper * cosine_table + lower * sine_table],
        axis=-1,
    )


def gather_all(values):
    inner = lax.all_gather(values, "exp", axis=0, tiled=False)
    return lax.all_gather(inner, "seq", axis=0, tiled=False)


def on_device(
    token_ids,
    cache_lengths,
    empty_blocks,
    expert_ids,
    embed_table,
    attn_gain,
    w_query,
    w_key,
    w_value,
    w_out,
    k_cache,
    v_cache,
    moe_gain,
    w_router,
    gate_pieces,
    up_pieces,
    down_pieces,
    shared_gate,
    shared_up,
    shared_down,
    final_gain,
    w_head,
):
    steps, requests = token_ids.shape
    tokens = steps * requests
    width = embed_table.shape[1]
    vocab_local = embed_table.shape[0]
    n_seq = lax.axis_size("seq")
    n_exp = lax.axis_size("exp")
    n_dev = n_seq * n_exp
    owner_index = lax.axis_index(("seq", "exp"))
    seq_index = lax.axis_index("seq")
    own_count = requests // n_exp
    own_start = lax.axis_index("exp") * own_count
    group = steps * own_count
    share = group // n_seq

    def permuted(values):
        rest = values.shape[2:]
        grouped = jnp.moveaxis(values.reshape((steps, n_exp, own_count) + rest), 1, 0)
        split = grouped.reshape((n_exp, n_seq, share) + rest)
        return jnp.swapaxes(split, 0, 1).reshape((tokens,) + rest)

    def natural(values):
        split = jnp.swapaxes(values.reshape(n_seq, n_exp, share), 0, 1)
        grouped = split.reshape(n_exp, steps, own_count)
        return jnp.moveaxis(grouped, 0, 1).reshape(steps, requests)

    local_ids = token_ids - owner_index * vocab_local
    held = (local_ids >= 0) & (local_ids < vocab_local)
    rows = jnp.take(embed_table, jnp.clip(local_ids, 0, vocab_local - 1), axis=0)
    rows = jnp.where(held[..., None], rows, jnp.zeros((), rows.dtype))
    rows = jnp.moveaxis(rows.reshape(steps, n_exp, own_count, width), 1, 0)
    arrived = lax.all_to_all(rows, "exp", 0, 0, tiled=True)
    row_part = jnp.sum(arrived.astype(jnp.float32), axis=0).astype(jnp.bfloat16)
    row_parts = lax.all_gather(row_part, "seq", axis=0, tiled=False)
    embedded = jnp.sum(row_parts.astype(jnp.float32), axis=0).reshape(group, width)

    attn_in = rms_scale(embedded, attn_gain).astype(jnp.bfloat16)
    own_lengths = lax.dynamic_slice_in_dim(cache_lengths, own_start, own_count, 0)
    places = (own_lengths[None, :] + jnp.arange(steps, dtype=jnp.int32)[:, None]).reshape(group)
    heads_here = w_query.shape[1] // HDIM

    def project(weight):
        return jnp.dot(attn_in, weight, preferred_element_type=jnp.float32).reshape(
            group, heads_here, HDIM
        )

    query_part = rotate(project(w_query), places).astype(jnp.bfloat16)
    key_part = rotate(project(w_key), places).astype(jnp.bfloat16)
    value_part = project(w_value).astype(jnp.bfloat16)
    every = lax.all_gather(
        jnp.stack([query_part, key_part, value_part], axis=0), "seq", axis=0, tiled=False
    )
    head_count = n_seq * heads_here
    every = jnp.moveaxis(every, 0, 2).reshape(3, steps, own_count, head_count, HDIM)
    queries = every[0]

    span = k_cache.shape[1]
    first_place = seq_index * span
    places_here = first_place + jnp.arange(span, dtype=jnp.int32)
    own_empty = lax.dynamic_slice_in_dim(empty_blocks, own_start, own_count, 0)
    local_blocks = lax.dynamic_slice_in_dim(own_empty, first_place // BLK, span // BLK, 1)
    blocked = jnp.broadcast_to(local_blocks[:, :, None], (own_count, span // BLK, BLK)).reshape(
        own_count, span
    )
    live_mask = ((places_here[None, :] < own_lengths[:, None]) & (blocked == 0))[None, :, None, :]
    cache_keys = k_cache.reshape(own_count, span, head_count, HDIM)
    cache_values = v_cache.reshape(own_count, span, head_count, HDIM)
    score_scale = 1.0 / math.sqrt(HDIM)
    cached = (
        jnp.einsum("trhd,rphd->trhp", queries, cache_keys, preferred_element_type=jnp.float32)
        * score_scale
    )
    local_top = jnp.max(jnp.where(live_mask, cached, negative), axis=3)
    local_weights = jnp.where(live_mask, jnp.exp(cached - local_top[..., None]), 0.0)
    local_totals = jnp.sum(local_weights, axis=3)
    local_mixture = jnp.einsum(
        "trhp,rphd->trhd",
        local_weights.astype(jnp.bfloat16),
        cache_values,
        preferred_element_type=jnp.float32,
    )

    def by_owner(values):
        rest = values.shape[3:]
        split = values.reshape((steps, own_count, n_seq, heads_here) + rest)
        return jnp.moveaxis(split, 2, 0).reshape(n_seq, -1)

    mix_len = group * heads_here * HDIM
    stat_len = group * heads_here
    packed = jnp.concatenate(
        [by_owner(local_mixture), by_owner(local_top), by_owner(local_totals)], axis=1
    )
    got = lax.all_to_all(packed, "seq", 0, 0, tiled=True)
    got_mixture = got[:, :mix_len].reshape(n_seq, steps, own_count, heads_here, HDIM)
    got_top = got[:, mix_len : mix_len + stat_len].reshape(n_seq, steps, own_count, heads_here)
    got_totals = got[:, mix_len + stat_len :].reshape(n_seq, steps, own_count, heads_here)

    own_queries = query_part.reshape(steps, own_count, heads_here, HDIM)
    own_keys = key_part.reshape(steps, own_count, heads_here, HDIM)
    own_values = value_part.reshape(steps, own_count, heads_here, HDIM)
    fresh_scores = (
        jnp.einsum("trhd,urhd->trhu", own_queries, own_keys, preferred_element_type=jnp.float32)
        * score_scale
    )
    causal = (jnp.arange(steps)[None, :] <= jnp.arange(steps)[:, None])[:, None, None, :]
    fresh_top = jnp.max(jnp.where(causal, fresh_scores, negative), axis=3)
    fresh_weights = jnp.where(causal, jnp.exp(fresh_scores - fresh_top[..., None]), 0.0)
    fresh_mixture = jnp.einsum(
        "trhu,urhd->trhd",
        fresh_weights.astype(jnp.bfloat16),
        own_values,
        preferred_element_type=jnp.float32,
    )
    top_score = jnp.maximum(jnp.max(got_top, axis=0), fresh_top)
    cache_factor = jnp.exp(got_top - top_score[None])
    fresh_factor = jnp.exp(fresh_top - top_score)
    totals = jnp.sum(got_totals * cache_factor, axis=0) + jnp.sum(fresh_weights, axis=3) * fresh_factor
    mixture = (
        jnp.sum(got_mixture * cache_factor[..., None], axis=0)
        + fresh_mixture * fresh_factor[..., None]
    )
    own_heads = (mixture / totals[..., None]).astype(jnp.bfloat16).reshape(
        group, heads_here * HDIM
    )

    attn_part = jnp.dot(own_heads, w_out, preferred_element_type=jnp.float32)
    attn_sum = jnp.sum(
        lax.all_to_all(attn_part.reshape(n_seq, share, width), "seq", 0, 0, tiled=True), axis=0
    )
    resid_share = lax.dynamic_slice_in_dim(embedded, seq_index * share, share, 0) + attn_sum
    moe_in = gather_all(rms_scale(resid_share, moe_gain).astype(jnp.bfloat16)).reshape(
        tokens, width
    )

    router = jax.nn.sigmoid(jnp.dot(moe_in, w_router, preferred_element_type=jnp.float32))
    expert_count = w_router.shape[1]
    chosen_ids = permuted(expert_ids)
    picked = chosen_ids[:, :, None] == jnp.arange(expert_count, dtype=jnp.int32)[None, None, :]
    chosen = jnp.sum(jnp.where(picked, router[:, None, :], 0.0), axis=2)
    gate_weights = chosen / jnp.sum(chosen, axis=1, keepdims=True)
    rows_here = gate_pieces.shape[0]
    row_expert = (owner_index * rows_here + jnp.arange(rows_here, dtype=jnp.int32)) // PIECES
    token_weight = jnp.sum(
        jnp.where(
            chosen_ids[None, :, :] == row_expert[:, None, None], gate_weights[None, :, :], 0.0
        ),
        axis=2,
    )
    gate_out = jnp.einsum("nd,jdf->jnf", moe_in, gate_pieces, preferred_element_type=jnp.float32)
    up_out = jnp.einsum("nd,jdf->jnf", moe_in, up_pieces, preferred_element_type=jnp.float32)
    expert_hidden = (jax.nn.silu(gate_out) * up_out).astype(jnp.bfloat16)
    expert_out = jnp.einsum(
        "jnf,jfd->jnd", expert_hidden, down_pieces, preferred_element_type=jnp.float32
    )
    routed = jnp.einsum("jn,jnd->nd", token_weight, expert_out)
    share_count = tokens // n_seq
    share_start = seq_index * share_count
    share_rows = lax.dynamic_slice_in_dim(moe_in, share_start, share_count, 0)
    shared_hidden = (
        jax.nn.silu(jnp.dot(share_rows, shared_gate, preferred_element_type=jnp.float32))
        * jnp.dot(share_rows, shared_up, preferred_element_type=jnp.float32)
    ).astype(jnp.bfloat16)
    shared_out = jnp.dot(shared_hidden, shared_down, preferred_element_type=jnp.float32)
    term_rows = lax.dynamic_update_slice_in_dim(
        routed,
        lax.dynamic_slice_in_dim(routed, share_start, share_count, 0) + shared_out,
        share_start,
        0,
    )

    term_sum = jnp.sum(
        lax.all_to_all(term_rows.reshape(n_dev, share, width), ("seq", "exp"), 0, 0, tiled=True),
        axis=0,
    )
    final_share = resid_share + term_sum
    norms_share = jnp.sqrt(jnp.mean(final_share * final_share, axis=-1))
    head_in = gather_all(rms_scale(final_share, final_gain).astype(jnp.bfloat16)).reshape(
        tokens, width
    )
    local_best = jnp.max(jnp.dot(head_in, w_head, preferred_element_type=jnp.float32), axis=-1)
    message = jnp.concatenate([local_best, norms_share], axis=0)
    heard = lax.all_to_all(
        jnp.broadcast_to(message[None, :], (n_dev, message.shape[0])),
        ("seq", "exp"),
        0,
        0,
        tiled=True,
    )
    greatest_logits = natural(jnp.max(heard[:, :tokens], axis=0))
    hidden_norms = natural(heard[:, tokens:].reshape(tokens))
    return (hidden_norms, greatest_logits)


def solution(mesh):
    in_specs = (
        P(),
        P(),
        P(),
        P(),
        P(("seq", "exp"), None),
        P(),
        P(None, "seq"),
        P(None, "seq"),
        P(None, "seq"),
        P("seq", None),
        P("exp", "seq", None),
        P("exp", "seq", None),
        P(),
        P(),
        P(("seq", "exp"), None, None),
        P(("seq", "exp"), None, None),
        P(("seq", "exp"), None, None),
        P(None, "exp"),
        P(None, "exp"),
        P("exp", None),
        P(),
        P(None, ("seq", "exp")),
    )
    out_specs = (P(), P())
    return jax.shard_map(
        on_device, mesh=mesh, in_specs=in_specs, out_specs=out_specs, check_vma=False
    )
```

```python
import math

import jax
import jax.numpy as jnp
from jax import lax
from jax.sharding import PartitionSpec as P

HDIM = 128
PIECES = 4
BLK = 16


epsilon = 1e-06
negative = -1e30


def rms_scale(values, scales):
    return values * lax.rsqrt(jnp.mean(values * values, axis=-1, keepdims=True) + epsilon) * scales


def rotate(values, places):
    half_width = values.shape[-1] // 2
    frequency = 10000.0 ** (-2.0 * jnp.arange(half_width, dtype=jnp.float32) / values.shape[-1])
    angles = places.astype(jnp.float32)[..., None, None] * frequency
    cosine_table = jnp.cos(angles)
    sine_table = jnp.sin(angles)
    lower = values[..., :half_width]
    upper = values[..., half_width:]
    return jnp.concatenate(
        [lower * cosine_table - upper * sine_table, upper * cosine_table + lower * sine_table],
        axis=-1,
    )


def gather_all(values):
    inner = lax.all_gather(values, "exp", axis=0, tiled=False)
    return lax.all_gather(inner, "seq", axis=0, tiled=False)


def on_device(
    token_ids,
    cache_lengths,
    empty_blocks,
    expert_ids,
    embed_table,
    attn_gain,
    w_query,
    w_key,
    w_value,
    w_out,
    k_cache,
    v_cache,
    moe_gain,
    w_router,
    gate_pieces,
    up_pieces,
    down_pieces,
    shared_gate,
    shared_up,
    shared_down,
    final_gain,
    w_head,
):
    steps, requests = token_ids.shape
    tokens = steps * requests
    width = embed_table.shape[1]
    vocab_local = embed_table.shape[0]
    n_seq = lax.axis_size("seq")
    n_exp = lax.axis_size("exp")
    n_dev = n_seq * n_exp
    owner_index = lax.axis_index(("seq", "exp"))
    seq_index = lax.axis_index("seq")
    own_count = requests // n_exp
    own_start = lax.axis_index("exp") * own_count
    group = steps * own_count
    share = group // n_seq

    def grouped(values):
        rest = values.shape[2:]
        by_group = jnp.moveaxis(values.reshape((steps, n_exp, own_count) + rest), 1, 0)
        return by_group.reshape((tokens,) + rest)


    def natural(values):
        split = jnp.swapaxes(values.reshape(n_seq, n_exp, share), 0, 1)
        grouped = split.reshape(n_exp, steps, own_count)
        return jnp.moveaxis(grouped, 0, 1).reshape(steps, requests)

    local_ids = token_ids - owner_index * vocab_local
    held = (local_ids >= 0) & (local_ids < vocab_local)
    rows = jnp.take(embed_table, jnp.clip(local_ids, 0, vocab_local - 1), axis=0)
    rows = jnp.where(held[..., None], rows, jnp.zeros((), rows.dtype))
    rows = jnp.moveaxis(rows.reshape(steps, n_exp, own_count, width), 1, 0)
    arrived = lax.all_to_all(rows, "exp", 0, 0, tiled=True)
    row_part = jnp.sum(arrived.astype(jnp.float32), axis=0).astype(jnp.bfloat16)
    row_parts = lax.all_gather(row_part, "seq", axis=0, tiled=False)
    embedded = jnp.sum(row_parts.astype(jnp.float32), axis=0).reshape(group, width)

    attn_in = rms_scale(embedded, attn_gain).astype(jnp.bfloat16)
    own_lengths = lax.dynamic_slice_in_dim(cache_lengths, own_start, own_count, 0)
    places = (own_lengths[None, :] + jnp.arange(steps, dtype=jnp.int32)[:, None]).reshape(group)
    heads_here = w_query.shape[1] // HDIM

    def project(weight):
        return jnp.dot(attn_in, weight, preferred_element_type=jnp.float32).reshape(
            group, heads_here, HDIM
        )

    query_part = rotate(project(w_query), places).astype(jnp.bfloat16)
    key_part = rotate(project(w_key), places).astype(jnp.bfloat16)
    value_part = project(w_value).astype(jnp.bfloat16)
    every = lax.all_gather(
        jnp.stack([query_part, key_part, value_part], axis=0), "seq", axis=0, tiled=False
    )
    head_count = n_seq * heads_here
    every = jnp.moveaxis(every, 0, 2).reshape(3, steps, own_count, head_count, HDIM)
    queries = every[0]

    span = k_cache.shape[1]
    first_place = seq_index * span
    places_here = first_place + jnp.arange(span, dtype=jnp.int32)
    own_empty = lax.dynamic_slice_in_dim(empty_blocks, own_start, own_count, 0)
    local_blocks = lax.dynamic_slice_in_dim(own_empty, first_place // BLK, span // BLK, 1)
    blocked = jnp.broadcast_to(local_blocks[:, :, None], (own_count, span // BLK, BLK)).reshape(
        own_count, span
    )
    live_mask = ((places_here[None, :] < own_lengths[:, None]) & (blocked == 0))[None, :, None, :]
    cache_keys = k_cache.reshape(own_count, span, head_count, HDIM)
    cache_values = v_cache.reshape(own_count, span, head_count, HDIM)
    score_scale = 1.0 / math.sqrt(HDIM)
    cached = (
        jnp.einsum("trhd,rphd->trhp", queries, cache_keys, preferred_element_type=jnp.float32)
        * score_scale
    )
    local_top = jnp.max(jnp.where(live_mask, cached, negative), axis=3)
    local_weights = jnp.where(live_mask, jnp.exp(cached - local_top[..., None]), 0.0)
    local_totals = jnp.sum(local_weights, axis=3)
    local_mixture = jnp.einsum(
        "trhp,rphd->trhd",
        local_weights.astype(jnp.bfloat16),
        cache_values,
        preferred_element_type=jnp.float32,
    )

    def by_owner(values):
        rest = values.shape[3:]
        split = values.reshape((steps, own_count, n_seq, heads_here) + rest)
        return jnp.moveaxis(split, 2, 0).reshape(n_seq, -1)

    mix_len = group * heads_here * HDIM
    stat_len = group * heads_here
    packed = jnp.concatenate(
        [by_owner(local_mixture), by_owner(local_top), by_owner(local_totals)], axis=1
    )
    got = lax.all_to_all(packed, "seq", 0, 0, tiled=True)
    got_mixture = got[:, :mix_len].reshape(n_seq, steps, own_count, heads_here, HDIM)
    got_top = got[:, mix_len : mix_len + stat_len].reshape(n_seq, steps, own_count, heads_here)
    got_totals = got[:, mix_len + stat_len :].reshape(n_seq, steps, own_count, heads_here)

    own_queries = query_part.reshape(steps, own_count, heads_here, HDIM)
    own_keys = key_part.reshape(steps, own_count, heads_here, HDIM)
    own_values = value_part.reshape(steps, own_count, heads_here, HDIM)
    fresh_scores = (
        jnp.einsum("trhd,urhd->trhu", own_queries, own_keys, preferred_element_type=jnp.float32)
        * score_scale
    )
    causal = (jnp.arange(steps)[None, :] <= jnp.arange(steps)[:, None])[:, None, None, :]
    fresh_top = jnp.max(jnp.where(causal, fresh_scores, negative), axis=3)
    fresh_weights = jnp.where(causal, jnp.exp(fresh_scores - fresh_top[..., None]), 0.0)
    fresh_mixture = jnp.einsum(
        "trhu,urhd->trhd",
        fresh_weights.astype(jnp.bfloat16),
        own_values,
        preferred_element_type=jnp.float32,
    )
    top_score = jnp.maximum(jnp.max(got_top, axis=0), fresh_top)
    cache_factor = jnp.exp(got_top - top_score[None])
    fresh_factor = jnp.exp(fresh_top - top_score)
    totals = jnp.sum(got_totals * cache_factor, axis=0) + jnp.sum(fresh_weights, axis=3) * fresh_factor
    mixture = (
        jnp.sum(got_mixture * cache_factor[..., None], axis=0)
        + fresh_mixture * fresh_factor[..., None]
    )
    own_heads = (mixture / totals[..., None]).astype(jnp.bfloat16).reshape(
        group, heads_here * HDIM
    )

    attn_part = jnp.dot(own_heads, w_out, preferred_element_type=jnp.float32)
    resid_group = embedded + jnp.sum(lax.all_gather(attn_part, "seq", axis=0, tiled=False), axis=0)
    resid_share = lax.dynamic_slice_in_dim(resid_group, seq_index * share, share, 0)
    moe_in = lax.all_gather(
        rms_scale(resid_group, moe_gain).astype(jnp.bfloat16), "exp", axis=0, tiled=True
    )

    router = jax.nn.sigmoid(jnp.dot(moe_in, w_router, preferred_element_type=jnp.float32))
    expert_count = w_router.shape[1]
    chosen_ids = grouped(expert_ids)
    picked = chosen_ids[:, :, None] == jnp.arange(expert_count, dtype=jnp.int32)[None, None, :]
    chosen = jnp.sum(jnp.where(picked, router[:, None, :], 0.0), axis=2)
    gate_weights = chosen / jnp.sum(chosen, axis=1, keepdims=True)
    rows_here = gate_pieces.shape[0]
    row_expert = (owner_index * rows_here + jnp.arange(rows_here, dtype=jnp.int32)) // PIECES
    token_weight = jnp.sum(
        jnp.where(
            chosen_ids[None, :, :] == row_expert[:, None, None], gate_weights[None, :, :], 0.0
        ),
        axis=2,
    )
    gate_out = jnp.einsum("nd,jdf->jnf", moe_in, gate_pieces, preferred_element_type=jnp.float32)
    up_out = jnp.einsum("nd,jdf->jnf", moe_in, up_pieces, preferred_element_type=jnp.float32)
    expert_hidden = (jax.nn.silu(gate_out) * up_out).astype(jnp.bfloat16)
    expert_out = jnp.einsum(
        "jnf,jfd->jnd", expert_hidden, down_pieces, preferred_element_type=jnp.float32
    )
    routed = jnp.einsum("jn,jnd->nd", token_weight, expert_out)
    share_count = tokens // n_seq
    share_start = seq_index * share_count
    share_rows = lax.dynamic_slice_in_dim(moe_in, share_start, share_count, 0)
    shared_hidden = (
        jax.nn.silu(jnp.dot(share_rows, shared_gate, preferred_element_type=jnp.float32))
        * jnp.dot(share_rows, shared_up, preferred_element_type=jnp.float32)
    ).astype(jnp.bfloat16)
    shared_out = jnp.dot(shared_hidden, shared_down, preferred_element_type=jnp.float32)
    term_rows = lax.dynamic_update_slice_in_dim(
        routed,
        lax.dynamic_slice_in_dim(routed, share_start, share_count, 0) + shared_out,
        share_start,
        0,
    )

    term_rows = jnp.swapaxes(term_rows.reshape(n_exp, n_seq, share, width), 0, 1)
    term_sum = jnp.sum(
        lax.all_to_all(
            term_rows.reshape(n_dev, share, width).astype(jnp.bfloat16),
            ("seq", "exp"),
            0,
            0,
            tiled=True,
        ).astype(jnp.float32),
        axis=0,
    )
    final_share = resid_share + term_sum
    norms_share = jnp.sqrt(jnp.mean(final_share * final_share, axis=-1))
    head_in = gather_all(rms_scale(final_share, final_gain).astype(jnp.bfloat16)).reshape(
        tokens, width
    )
    local_best = jnp.max(jnp.dot(head_in, w_head, preferred_element_type=jnp.float32), axis=-1)
    message = jnp.concatenate([local_best, norms_share], axis=0)
    heard = lax.all_to_all(
        jnp.broadcast_to(message[None, :], (n_dev, message.shape[0])),
        ("seq", "exp"),
        0,
        0,
        tiled=True,
    )
    greatest_logits = natural(jnp.max(heard[:, :tokens], axis=0))
    hidden_norms = natural(heard[:, tokens:].reshape(tokens))
    return (hidden_norms, greatest_logits)


def solution(mesh):
    in_specs = (
        P(),
        P(),
        P(),
        P(),
        P(("seq", "exp"), None),
        P(),
        P(None, "seq"),
        P(None, "seq"),
        P(None, "seq"),
        P("seq", None),
        P("exp", "seq", None),
        P("exp", "seq", None),
        P(),
        P(),
        P(("seq", "exp"), None, None),
        P(("seq", "exp"), None, None),
        P(("seq", "exp"), None, None),
        P(None, "exp"),
        P(None, "exp"),
        P("exp", None),
        P(),
        P(None, ("seq", "exp")),
    )
    out_specs = (P(), P())
    return jax.shard_map(
        on_device, mesh=mesh, in_specs=in_specs, out_specs=out_specs, check_vma=False
    )
```

```python
import math

import jax
import jax.numpy as jnp
from jax import lax
from jax.sharding import PartitionSpec as P

HDIM = 128
PIECES = 4
BLK = 16


epsilon = 1e-06
negative = -1e30


def rms_scale(values, scales):
    return values * lax.rsqrt(jnp.mean(values * values, axis=-1, keepdims=True) + epsilon) * scales


def rotate(values, places):
    half_width = values.shape[-1] // 2
    frequency = 10000.0 ** (-2.0 * jnp.arange(half_width, dtype=jnp.float32) / values.shape[-1])
    angles = places.astype(jnp.float32)[..., None, None] * frequency
    cosine_table = jnp.cos(angles)
    sine_table = jnp.sin(angles)
    lower = values[..., :half_width]
    upper = values[..., half_width:]
    return jnp.concatenate(
        [lower * cosine_table - upper * sine_table, upper * cosine_table + lower * sine_table],
        axis=-1,
    )


def gather_all(values):
    inner = lax.all_gather(values, "exp", axis=0, tiled=False)
    return lax.all_gather(inner, "seq", axis=0, tiled=False)


def on_device(
    token_ids,
    cache_lengths,
    empty_blocks,
    expert_ids,
    embed_table,
    attn_gain,
    w_query,
    w_key,
    w_value,
    w_out,
    k_cache,
    v_cache,
    moe_gain,
    w_router,
    gate_pieces,
    up_pieces,
    down_pieces,
    shared_gate,
    shared_up,
    shared_down,
    final_gain,
    w_head,
):
    steps, requests = token_ids.shape
    tokens = steps * requests
    width = embed_table.shape[1]
    vocab_local = embed_table.shape[0]
    n_seq = lax.axis_size("seq")
    n_exp = lax.axis_size("exp")
    n_dev = n_seq * n_exp
    owner_index = lax.axis_index(("seq", "exp"))
    seq_index = lax.axis_index("seq")
    own_count = requests // n_exp
    own_start = lax.axis_index("exp") * own_count
    group = steps * own_count
    share = group // n_seq

    def grouped(values):
        rest = values.shape[2:]
        by_group = jnp.moveaxis(values.reshape((steps, n_exp, own_count) + rest), 1, 0)
        return by_group.reshape((tokens,) + rest)


    def natural(values):
        split = jnp.swapaxes(values.reshape(n_seq, n_exp, share), 0, 1)
        grouped = split.reshape(n_exp, steps, own_count)
        return jnp.moveaxis(grouped, 0, 1).reshape(steps, requests)

    group_ids = jnp.moveaxis(token_ids.reshape(steps, n_exp, own_count), 1, 0)
    local_ids = group_ids - owner_index * vocab_local
    held = (local_ids >= 0) & (local_ids < vocab_local)
    rows = jnp.take(embed_table, jnp.clip(local_ids, 0, vocab_local - 1), axis=0)
    rows = jnp.where(held[..., None], rows, jnp.zeros((), rows.dtype))
    arrived = lax.all_to_all(rows, "exp", 0, 0, tiled=True)
    row_part = jnp.sum(arrived.astype(jnp.float32), axis=0).astype(jnp.bfloat16)
    row_parts = lax.all_gather(row_part, "seq", axis=0, tiled=False)
    embedded = jnp.sum(row_parts.astype(jnp.float32), axis=0).reshape(group, width)

    attn_in = rms_scale(embedded, attn_gain).astype(jnp.bfloat16)
    own_lengths = lax.dynamic_slice_in_dim(cache_lengths, own_start, own_count, 0)
    places = (own_lengths[None, :] + jnp.arange(steps, dtype=jnp.int32)[:, None]).reshape(group)
    heads_here = w_query.shape[1] // HDIM

    def project(weight):
        return jnp.dot(attn_in, weight, preferred_element_type=jnp.float32).reshape(
            group, heads_here, HDIM
        )

    query_part = rotate(project(w_query), places).astype(jnp.bfloat16)
    key_part = rotate(project(w_key), places).astype(jnp.bfloat16)
    value_part = project(w_value).astype(jnp.bfloat16)
    every = lax.all_gather(
        jnp.stack([query_part, key_part, value_part], axis=0), "seq", axis=0, tiled=False
    )
    head_count = n_seq * heads_here
    every = jnp.moveaxis(every, 0, 2).reshape(3, steps, own_count, head_count, HDIM)
    queries = every[0]

    span = k_cache.shape[1]
    first_place = seq_index * span
    places_here = first_place + jnp.arange(span, dtype=jnp.int32)
    own_empty = lax.dynamic_slice_in_dim(empty_blocks, own_start, own_count, 0)
    local_blocks = lax.dynamic_slice_in_dim(own_empty, first_place // BLK, span // BLK, 1)
    blocked = jnp.broadcast_to(local_blocks[:, :, None], (own_count, span // BLK, BLK)).reshape(
        own_count, span
    )
    live_mask = ((places_here[None, :] < own_lengths[:, None]) & (blocked == 0))[None, :, None, :]
    cache_keys = k_cache.reshape(own_count, span, head_count, HDIM)
    cache_values = v_cache.reshape(own_count, span, head_count, HDIM)
    score_scale = 1.0 / math.sqrt(HDIM)
    cached = (
        jnp.einsum("trhd,rphd->trhp", queries, cache_keys, preferred_element_type=jnp.float32)
        * score_scale
    )
    local_top = jnp.max(jnp.where(live_mask, cached, negative), axis=3)
    local_weights = jnp.where(live_mask, jnp.exp(cached - local_top[..., None]), 0.0)
    local_totals = jnp.sum(local_weights, axis=3)
    local_mixture = jnp.einsum(
        "trhp,rphd->trhd",
        local_weights.astype(jnp.bfloat16),
        cache_values,
        preferred_element_type=jnp.float32,
    )

    def by_owner(values):
        rest = values.shape[3:]
        split = values.reshape((steps, own_count, n_seq, heads_here) + rest)
        return jnp.moveaxis(split, 2, 0).reshape(n_seq, -1)

    mix_len = group * heads_here * HDIM
    stat_len = group * heads_here
    packed = jnp.concatenate(
        [by_owner(local_mixture), by_owner(local_top), by_owner(local_totals)], axis=1
    )
    got = lax.all_to_all(packed, "seq", 0, 0, tiled=True)
    got_mixture = got[:, :mix_len].reshape(n_seq, steps, own_count, heads_here, HDIM)
    got_top = got[:, mix_len : mix_len + stat_len].reshape(n_seq, steps, own_count, heads_here)
    got_totals = got[:, mix_len + stat_len :].reshape(n_seq, steps, own_count, heads_here)

    own_queries = query_part.reshape(steps, own_count, heads_here, HDIM)
    own_keys = key_part.reshape(steps, own_count, heads_here, HDIM)
    own_values = value_part.reshape(steps, own_count, heads_here, HDIM)
    fresh_scores = (
        jnp.einsum("trhd,urhd->trhu", own_queries, own_keys, preferred_element_type=jnp.float32)
        * score_scale
    )
    causal = (jnp.arange(steps)[None, :] <= jnp.arange(steps)[:, None])[:, None, None, :]
    fresh_top = jnp.max(jnp.where(causal, fresh_scores, negative), axis=3)
    fresh_weights = jnp.where(causal, jnp.exp(fresh_scores - fresh_top[..., None]), 0.0)
    fresh_mixture = jnp.einsum(
        "trhu,urhd->trhd",
        fresh_weights.astype(jnp.bfloat16),
        own_values,
        preferred_element_type=jnp.float32,
    )
    top_score = jnp.maximum(jnp.max(got_top, axis=0), fresh_top)
    cache_factor = jnp.exp(got_top - top_score[None])
    fresh_factor = jnp.exp(fresh_top - top_score)
    totals = jnp.sum(got_totals * cache_factor, axis=0) + jnp.sum(fresh_weights, axis=3) * fresh_factor
    mixture = (
        jnp.sum(got_mixture * cache_factor[..., None], axis=0)
        + fresh_mixture * fresh_factor[..., None]
    )
    own_heads = (mixture / totals[..., None]).astype(jnp.bfloat16).reshape(
        group, heads_here * HDIM
    )

    attn_part = jnp.dot(own_heads, w_out, preferred_element_type=jnp.float32)
    resid_group = embedded + jnp.sum(lax.all_gather(attn_part, "seq", axis=0, tiled=False), axis=0)
    resid_share = lax.dynamic_slice_in_dim(resid_group, seq_index * share, share, 0)
    moe_in = lax.all_gather(
        rms_scale(resid_group, moe_gain).astype(jnp.bfloat16), "exp", axis=0, tiled=True
    )

    router = jax.nn.sigmoid(jnp.dot(moe_in, w_router, preferred_element_type=jnp.float32))
    expert_count = w_router.shape[1]
    chosen_ids = grouped(expert_ids)
    picked = chosen_ids[:, :, None] == jnp.arange(expert_count, dtype=jnp.int32)[None, None, :]
    chosen = jnp.sum(jnp.where(picked, router[:, None, :], 0.0), axis=2)
    gate_weights = chosen / jnp.sum(chosen, axis=1, keepdims=True)
    rows_here = gate_pieces.shape[0]
    row_expert = (owner_index * rows_here + jnp.arange(rows_here, dtype=jnp.int32)) // PIECES
    token_weight = jnp.sum(
        jnp.where(
            chosen_ids[None, :, :] == row_expert[:, None, None], gate_weights[None, :, :], 0.0
        ),
        axis=2,
    )
    gate_out = jnp.einsum("nd,jdf->jnf", moe_in, gate_pieces, preferred_element_type=jnp.float32)
    up_out = jnp.einsum("nd,jdf->jnf", moe_in, up_pieces, preferred_element_type=jnp.float32)
    weighted_hidden = (jax.nn.silu(gate_out) * up_out * token_weight[:, :, None]).astype(
        jnp.bfloat16
    )
    routed = jnp.einsum(
        "jnf,jfd->nd", weighted_hidden, down_pieces, preferred_element_type=jnp.float32
    )
    share_count = tokens // n_seq
    share_start = seq_index * share_count
    share_rows = lax.dynamic_slice_in_dim(moe_in, share_start, share_count, 0)
    shared_hidden = (
        jax.nn.silu(jnp.dot(share_rows, shared_gate, preferred_element_type=jnp.float32))
        * jnp.dot(share_rows, shared_up, preferred_element_type=jnp.float32)
    ).astype(jnp.bfloat16)
    shared_out = jnp.dot(shared_hidden, shared_down, preferred_element_type=jnp.float32)
    term_rows = lax.dynamic_update_slice_in_dim(
        routed,
        lax.dynamic_slice_in_dim(routed, share_start, share_count, 0) + shared_out,
        share_start,
        0,
    )

    term_rows = jnp.swapaxes(term_rows.reshape(n_exp, n_seq, share, width), 0, 1)
    term_sum = jnp.sum(
        lax.all_to_all(
            term_rows.reshape(n_dev, share, width).astype(jnp.bfloat16),
            ("seq", "exp"),
            0,
            0,
            tiled=True,
        ).astype(jnp.float32),
        axis=0,
    )
    final_share = resid_share + term_sum
    norms_share = jnp.sqrt(jnp.mean(final_share * final_share, axis=-1))
    head_in = gather_all(rms_scale(final_share, final_gain).astype(jnp.bfloat16)).reshape(
        tokens, width
    )
    local_best = jnp.max(jnp.dot(head_in, w_head, preferred_element_type=jnp.float32), axis=-1)
    message = jnp.concatenate([local_best, norms_share], axis=0)
    heard = lax.all_to_all(
        jnp.broadcast_to(message[None, :], (n_dev, message.shape[0])),
        ("seq", "exp"),
        0,
        0,
        tiled=True,
    )
    greatest_logits = natural(jnp.max(heard[:, :tokens], axis=0))
    hidden_norms = natural(heard[:, tokens:].reshape(tokens))
    return (hidden_norms, greatest_logits)


def solution(mesh):
    in_specs = (
        P(),
        P(),
        P(),
        P(),
        P(("seq", "exp"), None),
        P(),
        P(None, "seq"),
        P(None, "seq"),
        P(None, "seq"),
        P("seq", None),
        P("exp", "seq", None),
        P("exp", "seq", None),
        P(),
        P(),
        P(("seq", "exp"), None, None),
        P(("seq", "exp"), None, None),
        P(("seq", "exp"), None, None),
        P(None, "exp"),
        P(None, "exp"),
        P("exp", None),
        P(),
        P(None, ("seq", "exp")),
    )
    out_specs = (P(), P())
    return jax.shard_map(
        on_device, mesh=mesh, in_specs=in_specs, out_specs=out_specs, check_vma=False
    )
```

```python
import math

import jax
import jax.numpy as jnp
from jax import lax
from jax.experimental import pallas as pl
from jax.experimental.pallas import tpu as pltpu
from jax.sharding import PartitionSpec as P

HDIM = 128
PIECES = 4
BLK = 16


epsilon = 1e-06
negative = -1e30


def rms_scale(values, scales):
    return values * lax.rsqrt(jnp.mean(values * values, axis=-1, keepdims=True) + epsilon) * scales


def rotate(values, places):
    half_width = values.shape[-1] // 2
    frequency = 10000.0 ** (-2.0 * jnp.arange(half_width, dtype=jnp.float32) / values.shape[-1])
    angles = places.astype(jnp.float32)[..., None, None] * frequency
    cosine_table = jnp.cos(angles)
    sine_table = jnp.sin(angles)
    lower = values[..., :half_width]
    upper = values[..., half_width:]
    return jnp.concatenate(
        [lower * cosine_table - upper * sine_table, upper * cosine_table + lower * sine_table],
        axis=-1,
    )


def gather_all(values):
    inner = lax.all_gather(values, "exp", axis=0, tiled=False)
    return lax.all_gather(inner, "seq", axis=0, tiled=False)


def experts_kernel(pieces, x_ref, weight_ref, gate_ref, up_ref, down_ref, sgate_ref, sup_ref, sdown_ref, mask_ref, out_ref):
    step = pl.program_id(0)

    @pl.when(step == 0)
    def _():
        out_ref[...] = jnp.zeros_like(out_ref)

    def one_piece(gate, up, down, scale):
        rows = x_ref[...]
        along = (((1,), (1,)), ((), ()))
        gate_out = lax.dot_general(rows, gate, along, preferred_element_type=jnp.float32)
        up_out = lax.dot_general(rows, up, along, preferred_element_type=jnp.float32)
        hidden = (gate_out * jax.nn.sigmoid(gate_out) * up_out * scale).astype(jnp.bfloat16)
        out_ref[...] += jnp.dot(hidden, down, preferred_element_type=jnp.float32)

    @pl.when(step < pieces)
    def _():
        one_piece(gate_ref[0], up_ref[0], down_ref[0], weight_ref[0])

    @pl.when(step == pieces)
    def _():
        one_piece(sgate_ref[...], sup_ref[...], sdown_ref[...], mask_ref[...])


def experts(rows, token_weight, gate_pieces, up_pieces, down_pieces, shared_gate, shared_up, shared_down, shared_mask):
    gate_pieces = jnp.swapaxes(gate_pieces, 1, 2)
    up_pieces = jnp.swapaxes(up_pieces, 1, 2)
    shared_gate = shared_gate.T
    shared_up = shared_up.T
    pieces, units, width = gate_pieces.shape
    count = rows.shape[0]
    last = pieces - 1

    def piece_map(step):
        return (jnp.minimum(step, last), 0, 0)

    weight_bytes = 2 * 3 * width * (pieces * units + shared_gate.shape[0])
    return pl.pallas_call(
        lambda *refs: experts_kernel(pieces, *refs),
        grid=(pieces + 1,),
        in_specs=[
            pl.BlockSpec((count, width), lambda step: (0, 0)),
            pl.BlockSpec((1, count, 1), piece_map),
            pl.BlockSpec((1, units, width), piece_map),
            pl.BlockSpec((1, units, width), piece_map),
            pl.BlockSpec((1, units, width), piece_map),
            pl.BlockSpec(shared_gate.shape, lambda step: (0, 0)),
            pl.BlockSpec(shared_up.shape, lambda step: (0, 0)),
            pl.BlockSpec(shared_down.shape, lambda step: (0, 0)),
            pl.BlockSpec((count, 1), lambda step: (0, 0)),
        ],
        out_specs=pl.BlockSpec((count, width), lambda step: (0, 0)),
        out_shape=jax.ShapeDtypeStruct((count, width), jnp.float32),
        cost_estimate=pl.CostEstimate(
            flops=6 * count * width * (pieces * units + shared_gate.shape[0]),
            transcendentals=count * (pieces * units + shared_gate.shape[0]),
            bytes_accessed=weight_bytes + 2 * count * width + 4 * count * width,
        ),
    )(rows, token_weight[:, :, None], gate_pieces, up_pieces, down_pieces, shared_gate, shared_up, shared_down, shared_mask)


def on_device(
    token_ids,
    cache_lengths,
    empty_blocks,
    expert_ids,
    embed_table,
    attn_gain,
    w_query,
    w_key,
    w_value,
    w_out,
    k_cache,
    v_cache,
    moe_gain,
    w_router,
    gate_pieces,
    up_pieces,
    down_pieces,
    shared_gate,
    shared_up,
    shared_down,
    final_gain,
    w_head,
):
    steps, requests = token_ids.shape
    tokens = steps * requests
    width = embed_table.shape[1]
    vocab_local = embed_table.shape[0]
    n_seq = lax.axis_size("seq")
    n_exp = lax.axis_size("exp")
    n_dev = n_seq * n_exp
    owner_index = lax.axis_index(("seq", "exp"))
    seq_index = lax.axis_index("seq")
    own_count = requests // n_exp
    own_start = lax.axis_index("exp") * own_count
    group = steps * own_count
    share = group // n_seq

    def grouped(values):
        rest = values.shape[2:]
        by_group = jnp.moveaxis(values.reshape((steps, n_exp, own_count) + rest), 1, 0)
        return by_group.reshape((tokens,) + rest)


    def natural(values):
        split = jnp.swapaxes(values.reshape(n_seq, n_exp, share), 0, 1)
        grouped = split.reshape(n_exp, steps, own_count)
        return jnp.moveaxis(grouped, 0, 1).reshape(steps, requests)

    group_ids = jnp.moveaxis(token_ids.reshape(steps, n_exp, own_count), 1, 0)
    local_ids = group_ids - owner_index * vocab_local
    held = (local_ids >= 0) & (local_ids < vocab_local)
    rows = jnp.take(embed_table, jnp.clip(local_ids, 0, vocab_local - 1), axis=0)
    rows = jnp.where(held[..., None], rows, jnp.zeros((), rows.dtype))
    arrived = lax.all_to_all(rows, "exp", 0, 0, tiled=True)
    row_part = jnp.sum(arrived.astype(jnp.float32), axis=0).astype(jnp.bfloat16)
    row_parts = lax.all_gather(row_part, "seq", axis=0, tiled=False)
    embedded = jnp.sum(row_parts.astype(jnp.float32), axis=0).reshape(group, width)

    attn_in = rms_scale(embedded, attn_gain).astype(jnp.bfloat16)
    own_lengths = lax.dynamic_slice_in_dim(cache_lengths, own_start, own_count, 0)
    places = (own_lengths[None, :] + jnp.arange(steps, dtype=jnp.int32)[:, None]).reshape(group)
    heads_here = w_query.shape[1] // HDIM

    def project(weight):
        return jnp.dot(attn_in, weight, preferred_element_type=jnp.float32).reshape(
            group, heads_here, HDIM
        )

    query_part = rotate(project(w_query), places).astype(jnp.bfloat16)
    key_part = rotate(project(w_key), places).astype(jnp.bfloat16)
    value_part = project(w_value).astype(jnp.bfloat16)
    every = lax.all_gather(
        jnp.stack([query_part, key_part, value_part], axis=0), "seq", axis=0, tiled=False
    )
    head_count = n_seq * heads_here
    every = jnp.moveaxis(every, 0, 2).reshape(3, steps, own_count, head_count, HDIM)
    queries = every[0]

    span = k_cache.shape[1]
    first_place = seq_index * span
    places_here = first_place + jnp.arange(span, dtype=jnp.int32)
    own_empty = lax.dynamic_slice_in_dim(empty_blocks, own_start, own_count, 0)
    local_blocks = lax.dynamic_slice_in_dim(own_empty, first_place // BLK, span // BLK, 1)
    blocked = jnp.broadcast_to(local_blocks[:, :, None], (own_count, span // BLK, BLK)).reshape(
        own_count, span
    )
    live_mask = ((places_here[None, :] < own_lengths[:, None]) & (blocked == 0))[None, :, None, :]
    cache_keys = k_cache.reshape(own_count, span, head_count, HDIM)
    cache_values = v_cache.reshape(own_count, span, head_count, HDIM)
    score_scale = 1.0 / math.sqrt(HDIM)
    cached = (
        jnp.einsum("trhd,rphd->trhp", queries, cache_keys, preferred_element_type=jnp.float32)
        * score_scale
    )
    local_top = jnp.max(jnp.where(live_mask, cached, negative), axis=3)
    local_weights = jnp.where(live_mask, jnp.exp(cached - local_top[..., None]), 0.0)
    local_totals = jnp.sum(local_weights, axis=3)
    local_mixture = jnp.einsum(
        "trhp,rphd->trhd",
        local_weights.astype(jnp.bfloat16),
        cache_values,
        preferred_element_type=jnp.float32,
    )

    def by_owner(values):
        rest = values.shape[3:]
        split = values.reshape((steps, own_count, n_seq, heads_here) + rest)
        return jnp.moveaxis(split, 2, 0).reshape(n_seq, -1)

    mix_len = group * heads_here * HDIM
    stat_len = group * heads_here
    packed = jnp.concatenate(
        [by_owner(local_mixture), by_owner(local_top), by_owner(local_totals)], axis=1
    )
    got = lax.all_to_all(packed, "seq", 0, 0, tiled=True)
    got_mixture = got[:, :mix_len].reshape(n_seq, steps, own_count, heads_here, HDIM)
    got_top = got[:, mix_len : mix_len + stat_len].reshape(n_seq, steps, own_count, heads_here)
    got_totals = got[:, mix_len + stat_len :].reshape(n_seq, steps, own_count, heads_here)

    own_queries = query_part.reshape(steps, own_count, heads_here, HDIM)
    own_keys = key_part.reshape(steps, own_count, heads_here, HDIM)
    own_values = value_part.reshape(steps, own_count, heads_here, HDIM)
    fresh_scores = (
        jnp.einsum("trhd,urhd->trhu", own_queries, own_keys, preferred_element_type=jnp.float32)
        * score_scale
    )
    causal = (jnp.arange(steps)[None, :] <= jnp.arange(steps)[:, None])[:, None, None, :]
    fresh_top = jnp.max(jnp.where(causal, fresh_scores, negative), axis=3)
    fresh_weights = jnp.where(causal, jnp.exp(fresh_scores - fresh_top[..., None]), 0.0)
    fresh_mixture = jnp.einsum(
        "trhu,urhd->trhd",
        fresh_weights.astype(jnp.bfloat16),
        own_values,
        preferred_element_type=jnp.float32,
    )
    top_score = jnp.maximum(jnp.max(got_top, axis=0), fresh_top)
    cache_factor = jnp.exp(got_top - top_score[None])
    fresh_factor = jnp.exp(fresh_top - top_score)
    totals = jnp.sum(got_totals * cache_factor, axis=0) + jnp.sum(fresh_weights, axis=3) * fresh_factor
    mixture = (
        jnp.sum(got_mixture * cache_factor[..., None], axis=0)
        + fresh_mixture * fresh_factor[..., None]
    )
    own_heads = (mixture / totals[..., None]).astype(jnp.bfloat16).reshape(
        group, heads_here * HDIM
    )

    attn_part = jnp.dot(own_heads, w_out, preferred_element_type=jnp.float32)
    resid_group = embedded + jnp.sum(lax.all_gather(attn_part, "seq", axis=0, tiled=False), axis=0)
    resid_share = lax.dynamic_slice_in_dim(resid_group, seq_index * share, share, 0)
    moe_in = lax.all_gather(
        rms_scale(resid_group, moe_gain).astype(jnp.bfloat16), "exp", axis=0, tiled=True
    )

    router = jax.nn.sigmoid(jnp.dot(moe_in, w_router, preferred_element_type=jnp.float32))
    expert_count = w_router.shape[1]
    chosen_ids = grouped(expert_ids)
    picked = chosen_ids[:, :, None] == jnp.arange(expert_count, dtype=jnp.int32)[None, None, :]
    chosen = jnp.sum(jnp.where(picked, router[:, None, :], 0.0), axis=2)
    gate_weights = chosen / jnp.sum(chosen, axis=1, keepdims=True)
    rows_here = gate_pieces.shape[0]
    row_expert = (owner_index * rows_here + jnp.arange(rows_here, dtype=jnp.int32)) // PIECES
    token_weight = jnp.sum(
        jnp.where(
            chosen_ids[None, :, :] == row_expert[:, None, None], gate_weights[None, :, :], 0.0
        ),
        axis=2,
    )
    share_count = tokens // n_seq
    share_start = seq_index * share_count
    token_place = jnp.arange(tokens, dtype=jnp.int32)
    shared_mask = (
        (token_place >= share_start) & (token_place < share_start + share_count)
    ).astype(jnp.float32)[:, None]
    term_rows = experts(
        moe_in, token_weight, gate_pieces, up_pieces, down_pieces,
        shared_gate, shared_up, shared_down, shared_mask,
    )

    term_rows = jnp.swapaxes(term_rows.reshape(n_exp, n_seq, share, width), 0, 1)
    term_sum = jnp.sum(
        lax.all_to_all(
            term_rows.reshape(n_dev, share, width).astype(jnp.bfloat16),
            ("seq", "exp"),
            0,
            0,
            tiled=True,
        ).astype(jnp.float32),
        axis=0,
    )
    final_share = resid_share + term_sum
    norms_share = jnp.sqrt(jnp.mean(final_share * final_share, axis=-1))
    head_in = gather_all(rms_scale(final_share, final_gain).astype(jnp.bfloat16)).reshape(
        tokens, width
    )
    local_best = jnp.max(jnp.dot(head_in, w_head, preferred_element_type=jnp.float32), axis=-1)
    message = jnp.concatenate([local_best, norms_share], axis=0)
    heard = lax.all_to_all(
        jnp.broadcast_to(message[None, :], (n_dev, message.shape[0])),
        ("seq", "exp"),
        0,
        0,
        tiled=True,
    )
    greatest_logits = natural(jnp.max(heard[:, :tokens], axis=0))
    hidden_norms = natural(heard[:, tokens:].reshape(tokens))
    return (hidden_norms, greatest_logits)


def solution(mesh):
    in_specs = (
        P(),
        P(),
        P(),
        P(),
        P(("seq", "exp"), None),
        P(),
        P(None, "seq"),
        P(None, "seq"),
        P(None, "seq"),
        P("seq", None),
        P("exp", "seq", None),
        P("exp", "seq", None),
        P(),
        P(),
        P(("seq", "exp"), None, None),
        P(("seq", "exp"), None, None),
        P(("seq", "exp"), None, None),
        P(None, "exp"),
        P(None, "exp"),
        P("exp", None),
        P(),
        P(None, ("seq", "exp")),
    )
    out_specs = (P(), P())
    return jax.shard_map(
        on_device, mesh=mesh, in_specs=in_specs, out_specs=out_specs, check_vma=False
    )
```

```python
import math

import jax
import jax.numpy as jnp
from jax import lax
from jax.experimental import pallas as pl
from jax.experimental.pallas import tpu as pltpu
from jax.sharding import PartitionSpec as P

HDIM = 128
PIECES = 4
BLK = 16


epsilon = 1e-06
negative = -1e30


def rms_scale(values, scales):
    return values * lax.rsqrt(jnp.mean(values * values, axis=-1, keepdims=True) + epsilon) * scales


def rotate(values, places):
    half_width = values.shape[-1] // 2
    frequency = 10000.0 ** (-2.0 * jnp.arange(half_width, dtype=jnp.float32) / values.shape[-1])
    angles = places.astype(jnp.float32)[..., None, None] * frequency
    cosine_table = jnp.cos(angles)
    sine_table = jnp.sin(angles)
    lower = values[..., :half_width]
    upper = values[..., half_width:]
    return jnp.concatenate(
        [lower * cosine_table - upper * sine_table, upper * cosine_table + lower * sine_table],
        axis=-1,
    )


def gather_all(values):
    inner = lax.all_gather(values, "exp", axis=0, tiled=False)
    return lax.all_gather(inner, "seq", axis=0, tiled=False)


def experts_kernel(pieces, x_ref, weight_ref, gate_ref, up_ref, down_ref, sgate_ref, sup_ref, sdown_ref, out_ref):
    step = pl.program_id(0)

    @pl.when(step == 0)
    def _():
        out_ref[...] = jnp.zeros_like(out_ref)

    def one_piece(gate, up, down, scale):
        rows = x_ref[...]
        along = (((1,), (1,)), ((), ()))
        gate_out = lax.dot_general(rows, gate, along, preferred_element_type=jnp.float32)
        up_out = lax.dot_general(rows, up, along, preferred_element_type=jnp.float32)
        hidden = (gate_out * jax.nn.sigmoid(gate_out) * up_out * scale).astype(jnp.bfloat16)
        out_ref[...] += jnp.dot(hidden, down, preferred_element_type=jnp.float32)

    table = weight_ref[...]
    column = lax.broadcasted_iota(jnp.int32, table.shape, 1)
    scale = jnp.sum(jnp.where(column == step, table, 0.0), axis=1, keepdims=True)

    @pl.when(step < pieces)
    def _():
        one_piece(gate_ref[0], up_ref[0], down_ref[0], scale)

    @pl.when(step == pieces)
    def _():
        one_piece(sgate_ref[...], sup_ref[...], sdown_ref[...], scale)


def experts(rows, weight_table, gate_pieces, up_pieces, down_pieces, shared_gate, shared_up, shared_down):
    gate_pieces = jnp.swapaxes(gate_pieces, 1, 2)
    up_pieces = jnp.swapaxes(up_pieces, 1, 2)
    shared_gate = shared_gate.T
    shared_up = shared_up.T
    pieces, units, width = gate_pieces.shape
    count = rows.shape[0]
    last = pieces - 1

    def piece_map(step):
        return (jnp.minimum(step, last), 0, 0)

    weight_bytes = 2 * 3 * width * (pieces * units + shared_gate.shape[0])
    return pl.pallas_call(
        lambda *refs: experts_kernel(pieces, *refs),
        grid=(pieces + 1,),
        in_specs=[
            pl.BlockSpec((count, width), lambda step: (0, 0)),
            pl.BlockSpec(weight_table.shape, lambda step: (0, 0)),
            pl.BlockSpec((1, units, width), piece_map),
            pl.BlockSpec((1, units, width), piece_map),
            pl.BlockSpec((1, units, width), piece_map),
            pl.BlockSpec(shared_gate.shape, lambda step: (0, 0)),
            pl.BlockSpec(shared_up.shape, lambda step: (0, 0)),
            pl.BlockSpec(shared_down.shape, lambda step: (0, 0)),
        ],
        out_specs=pl.BlockSpec((count, width), lambda step: (0, 0)),
        out_shape=jax.ShapeDtypeStruct((count, width), jnp.float32),
        cost_estimate=pl.CostEstimate(
            flops=6 * count * width * (pieces * units + shared_gate.shape[0]),
            transcendentals=count * (pieces * units + shared_gate.shape[0]),
            bytes_accessed=weight_bytes + 2 * count * width + 4 * count * width,
        ),
    )(rows, weight_table, gate_pieces, up_pieces, down_pieces, shared_gate, shared_up, shared_down)


def on_device(
    token_ids,
    cache_lengths,
    empty_blocks,
    expert_ids,
    embed_table,
    attn_gain,
    w_query,
    w_key,
    w_value,
    w_out,
    k_cache,
    v_cache,
    moe_gain,
    w_router,
    gate_pieces,
    up_pieces,
    down_pieces,
    shared_gate,
    shared_up,
    shared_down,
    final_gain,
    w_head,
):
    steps, requests = token_ids.shape
    tokens = steps * requests
    width = embed_table.shape[1]
    vocab_local = embed_table.shape[0]
    n_seq = lax.axis_size("seq")
    n_exp = lax.axis_size("exp")
    n_dev = n_seq * n_exp
    owner_index = lax.axis_index(("seq", "exp"))
    seq_index = lax.axis_index("seq")
    own_count = requests // n_exp
    own_start = lax.axis_index("exp") * own_count
    group = steps * own_count
    share = group // n_seq

    def grouped(values):
        rest = values.shape[2:]
        by_group = jnp.moveaxis(values.reshape((steps, n_exp, own_count) + rest), 1, 0)
        return by_group.reshape((tokens,) + rest)


    def natural(values):
        split = jnp.swapaxes(values.reshape(n_seq, n_exp, share), 0, 1)
        grouped = split.reshape(n_exp, steps, own_count)
        return jnp.moveaxis(grouped, 0, 1).reshape(steps, requests)

    group_ids = jnp.moveaxis(token_ids.reshape(steps, n_exp, own_count), 1, 0)
    local_ids = group_ids - owner_index * vocab_local
    held = (local_ids >= 0) & (local_ids < vocab_local)
    rows = jnp.take(embed_table, jnp.clip(local_ids, 0, vocab_local - 1), axis=0)
    rows = jnp.where(held[..., None], rows, jnp.zeros((), rows.dtype))
    arrived = lax.all_to_all(rows, "exp", 0, 0, tiled=True)
    row_part = jnp.sum(arrived.astype(jnp.float32), axis=0).astype(jnp.bfloat16)
    row_parts = lax.all_gather(row_part, "seq", axis=0, tiled=False)
    embedded = jnp.sum(row_parts.astype(jnp.float32), axis=0).reshape(group, width)

    attn_in = rms_scale(embedded, attn_gain).astype(jnp.bfloat16)
    own_lengths = lax.dynamic_slice_in_dim(cache_lengths, own_start, own_count, 0)
    places = (own_lengths[None, :] + jnp.arange(steps, dtype=jnp.int32)[:, None]).reshape(group)
    heads_here = w_query.shape[1] // HDIM

    def project(weight):
        return jnp.dot(attn_in, weight, preferred_element_type=jnp.float32).reshape(
            group, heads_here, HDIM
        )

    query_part = rotate(project(w_query), places).astype(jnp.bfloat16)
    key_part = rotate(project(w_key), places).astype(jnp.bfloat16)
    value_part = project(w_value).astype(jnp.bfloat16)
    every = lax.all_gather(
        jnp.stack([query_part, key_part, value_part], axis=0), "seq", axis=0, tiled=False
    )
    head_count = n_seq * heads_here
    every = jnp.moveaxis(every, 0, 2).reshape(3, steps, own_count, head_count, HDIM)
    queries = every[0]

    span = k_cache.shape[1]
    first_place = seq_index * span
    places_here = first_place + jnp.arange(span, dtype=jnp.int32)
    own_empty = lax.dynamic_slice_in_dim(empty_blocks, own_start, own_count, 0)
    local_blocks = lax.dynamic_slice_in_dim(own_empty, first_place // BLK, span // BLK, 1)
    blocked = jnp.broadcast_to(local_blocks[:, :, None], (own_count, span // BLK, BLK)).reshape(
        own_count, span
    )
    live_mask = ((places_here[None, :] < own_lengths[:, None]) & (blocked == 0))[None, :, None, :]
    cache_keys = k_cache.reshape(own_count, span, head_count, HDIM)
    cache_values = v_cache.reshape(own_count, span, head_count, HDIM)
    score_scale = 1.0 / math.sqrt(HDIM)
    cached = (
        jnp.einsum("trhd,rphd->trhp", queries, cache_keys, preferred_element_type=jnp.float32)
        * score_scale
    )
    local_top = jnp.max(jnp.where(live_mask, cached, negative), axis=3)
    local_weights = jnp.where(live_mask, jnp.exp(cached - local_top[..., None]), 0.0)
    local_totals = jnp.sum(local_weights, axis=3)
    local_mixture = jnp.einsum(
        "trhp,rphd->trhd",
        local_weights.astype(jnp.bfloat16),
        cache_values,
        preferred_element_type=jnp.float32,
    )

    def by_owner(values):
        rest = values.shape[3:]
        split = values.reshape((steps, own_count, n_seq, heads_here) + rest)
        return jnp.moveaxis(split, 2, 0).reshape(n_seq, -1)

    mix_len = group * heads_here * HDIM
    stat_len = group * heads_here
    packed = jnp.concatenate(
        [by_owner(local_mixture), by_owner(local_top), by_owner(local_totals)], axis=1
    )
    got = lax.all_to_all(packed, "seq", 0, 0, tiled=True)
    got_mixture = got[:, :mix_len].reshape(n_seq, steps, own_count, heads_here, HDIM)
    got_top = got[:, mix_len : mix_len + stat_len].reshape(n_seq, steps, own_count, heads_here)
    got_totals = got[:, mix_len + stat_len :].reshape(n_seq, steps, own_count, heads_here)

    own_queries = query_part.reshape(steps, own_count, heads_here, HDIM)
    own_keys = key_part.reshape(steps, own_count, heads_here, HDIM)
    own_values = value_part.reshape(steps, own_count, heads_here, HDIM)
    fresh_scores = (
        jnp.einsum("trhd,urhd->trhu", own_queries, own_keys, preferred_element_type=jnp.float32)
        * score_scale
    )
    causal = (jnp.arange(steps)[None, :] <= jnp.arange(steps)[:, None])[:, None, None, :]
    fresh_top = jnp.max(jnp.where(causal, fresh_scores, negative), axis=3)
    fresh_weights = jnp.where(causal, jnp.exp(fresh_scores - fresh_top[..., None]), 0.0)
    fresh_mixture = jnp.einsum(
        "trhu,urhd->trhd",
        fresh_weights.astype(jnp.bfloat16),
        own_values,
        preferred_element_type=jnp.float32,
    )
    top_score = jnp.maximum(jnp.max(got_top, axis=0), fresh_top)
    cache_factor = jnp.exp(got_top - top_score[None])
    fresh_factor = jnp.exp(fresh_top - top_score)
    totals = jnp.sum(got_totals * cache_factor, axis=0) + jnp.sum(fresh_weights, axis=3) * fresh_factor
    mixture = (
        jnp.sum(got_mixture * cache_factor[..., None], axis=0)
        + fresh_mixture * fresh_factor[..., None]
    )
    own_heads = (mixture / totals[..., None]).astype(jnp.bfloat16).reshape(
        group, heads_here * HDIM
    )

    attn_part = jnp.dot(own_heads, w_out, preferred_element_type=jnp.float32)
    attn_parts = lax.all_gather(attn_part.astype(jnp.bfloat16), "seq", axis=0, tiled=False)
    resid_group = embedded + jnp.sum(attn_parts.astype(jnp.float32), axis=0)
    resid_share = lax.dynamic_slice_in_dim(resid_group, seq_index * share, share, 0)
    moe_in = lax.all_gather(
        rms_scale(resid_group, moe_gain).astype(jnp.bfloat16), "exp", axis=0, tiled=True
    )

    router = jax.nn.sigmoid(jnp.dot(moe_in, w_router, preferred_element_type=jnp.float32))
    expert_count = w_router.shape[1]
    chosen_ids = grouped(expert_ids)
    picked = chosen_ids[:, :, None] == jnp.arange(expert_count, dtype=jnp.int32)[None, None, :]
    chosen = jnp.sum(jnp.where(picked, router[:, None, :], 0.0), axis=2)
    gate_weights = chosen / jnp.sum(chosen, axis=1, keepdims=True)
    rows_here = gate_pieces.shape[0]
    row_expert = (owner_index * rows_here + jnp.arange(rows_here, dtype=jnp.int32)) // PIECES
    token_weight = jnp.sum(
        jnp.where(
            chosen_ids[:, :, None] == row_expert[None, None, :], gate_weights[:, :, None], 0.0
        ),
        axis=1,
    )
    share_count = tokens // n_seq
    share_start = seq_index * share_count
    token_place = jnp.arange(tokens, dtype=jnp.int32)
    shared_mask = (
        (token_place >= share_start) & (token_place < share_start + share_count)
    ).astype(jnp.float32)[:, None]
    lanes = -(-(rows_here + 1) // 128) * 128
    weight_table = jnp.pad(
        jnp.concatenate([token_weight, shared_mask], axis=1), ((0, 0), (0, lanes - rows_here - 1))
    )
    term_rows = experts(
        moe_in, weight_table, gate_pieces, up_pieces, down_pieces,
        shared_gate, shared_up, shared_down,
    )

    term_rows = jnp.swapaxes(term_rows.reshape(n_exp, n_seq, share, width), 0, 1)
    term_sum = jnp.sum(
        lax.all_to_all(
            term_rows.reshape(n_dev, share, width).astype(jnp.bfloat16),
            ("seq", "exp"),
            0,
            0,
            tiled=True,
        ).astype(jnp.float32),
        axis=0,
    )
    final_share = resid_share + term_sum
    norms_share = jnp.sqrt(jnp.mean(final_share * final_share, axis=-1))
    head_share = rms_scale(final_share, final_gain).astype(jnp.bfloat16)
    rounds = n_exp.bit_length() - 1
    if n_exp == 1 << rounds:
        for level in reversed(range(rounds)):
            partner = [(i, i ^ (1 << level)) for i in range(n_exp)]
            head_share = jnp.concatenate([head_share, lax.ppermute(head_share, "exp", partner)], 0)
        head_in = lax.all_gather(head_share, "seq", axis=0, tiled=False).reshape(tokens, width)
        local_best = jnp.max(jnp.dot(head_in, w_head, preferred_element_type=jnp.float32), axis=-1)
        flipped = jnp.arange(n_exp, dtype=jnp.int32) ^ lax.axis_index("exp")
        block = sum(((flipped >> bit) & 1) << (rounds - 1 - bit) for bit in range(rounds))
        local_best = jnp.take(local_best.reshape(n_seq, n_exp, share), block, axis=1).reshape(tokens)
    else:
        head_in = gather_all(head_share).reshape(tokens, width)
        local_best = jnp.max(jnp.dot(head_in, w_head, preferred_element_type=jnp.float32), axis=-1)
    message = jnp.concatenate([local_best, norms_share], axis=0)
    heard = lax.all_to_all(
        jnp.broadcast_to(message[None, :], (n_dev, message.shape[0])),
        ("seq", "exp"),
        0,
        0,
        tiled=True,
    )
    greatest_logits = natural(jnp.max(heard[:, :tokens], axis=0))
    hidden_norms = natural(heard[:, tokens:].reshape(tokens))
    return (hidden_norms, greatest_logits)


def solution(mesh):
    in_specs = (
        P(),
        P(),
        P(),
        P(),
        P(("seq", "exp"), None),
        P(),
        P(None, "seq"),
        P(None, "seq"),
        P(None, "seq"),
        P("seq", None),
        P("exp", "seq", None),
        P("exp", "seq", None),
        P(),
        P(),
        P(("seq", "exp"), None, None),
        P(("seq", "exp"), None, None),
        P(("seq", "exp"), None, None),
        P(None, "exp"),
        P(None, "exp"),
        P("exp", None),
        P(),
        P(None, ("seq", "exp")),
    )
    out_specs = (P(), P())
    return jax.shard_map(
        on_device, mesh=mesh, in_specs=in_specs, out_specs=out_specs, check_vma=False
    )
```

```python
import math

import jax
import jax.numpy as jnp
from jax import lax
from jax.experimental import pallas as pl
from jax.experimental.pallas import tpu as pltpu
from jax.sharding import PartitionSpec as P

HDIM = 128
PIECES = 4
BLK = 16


epsilon = 1e-06
negative = -1e30


def rms_scale(values, scales):
    return values * lax.rsqrt(jnp.mean(values * values, axis=-1, keepdims=True) + epsilon) * scales


def rotate(values, places):
    half_width = values.shape[-1] // 2
    frequency = 10000.0 ** (-2.0 * jnp.arange(half_width, dtype=jnp.float32) / values.shape[-1])
    angles = places.astype(jnp.float32)[..., None, None] * frequency
    cosine_table = jnp.cos(angles)
    sine_table = jnp.sin(angles)
    lower = values[..., :half_width]
    upper = values[..., half_width:]
    return jnp.concatenate(
        [lower * cosine_table - upper * sine_table, upper * cosine_table + lower * sine_table],
        axis=-1,
    )


def gather_all(values):
    inner = lax.all_gather(values, "exp", axis=0, tiled=False)
    return lax.all_gather(inner, "seq", axis=0, tiled=False)


def experts_kernel(pieces, x_ref, weight_ref, gate_ref, up_ref, down_ref, sgate_ref, sup_ref, sdown_ref, out_ref, total_ref):
    step = pl.program_id(0)

    @pl.when(step == 0)
    def _():
        total_ref[...] = jnp.zeros_like(total_ref)

    def one_piece(gate, up, down, scale):
        rows = x_ref[...]
        along = (((1,), (1,)), ((), ()))
        gate_out = lax.dot_general(rows, gate, along, preferred_element_type=jnp.float32)
        up_out = lax.dot_general(rows, up, along, preferred_element_type=jnp.float32)
        hidden = (gate_out * jax.nn.sigmoid(gate_out) * up_out * scale).astype(jnp.bfloat16)
        total_ref[...] += jnp.dot(hidden, down, preferred_element_type=jnp.float32)

    table = weight_ref[...]
    column = lax.broadcasted_iota(jnp.int32, table.shape, 1)
    scale = jnp.sum(jnp.where(column == step, table, 0.0), axis=1, keepdims=True)

    @pl.when(step < pieces)
    def _():
        one_piece(gate_ref[0], up_ref[0], down_ref[0], scale)

    @pl.when(step == pieces)
    def _():
        one_piece(sgate_ref[...], sup_ref[...], sdown_ref[...], scale)
        out_ref[...] = total_ref[...].astype(out_ref.dtype)


def experts(rows, weight_table, gate_pieces, up_pieces, down_pieces, shared_gate, shared_up, shared_down):
    gate_pieces = jnp.swapaxes(gate_pieces, 1, 2)
    up_pieces = jnp.swapaxes(up_pieces, 1, 2)
    shared_gate = shared_gate.T
    shared_up = shared_up.T
    pieces, units, width = gate_pieces.shape
    count = rows.shape[0]
    last = pieces - 1

    def piece_map(step):
        return (jnp.minimum(step, last), 0, 0)

    weight_bytes = 2 * 3 * width * (pieces * units + shared_gate.shape[0])
    return pl.pallas_call(
        lambda *refs: experts_kernel(pieces, *refs),
        grid=(pieces + 1,),
        in_specs=[
            pl.BlockSpec((count, width), lambda step: (0, 0)),
            pl.BlockSpec(weight_table.shape, lambda step: (0, 0)),
            pl.BlockSpec((1, units, width), piece_map),
            pl.BlockSpec((1, units, width), piece_map),
            pl.BlockSpec((1, units, width), piece_map),
            pl.BlockSpec(shared_gate.shape, lambda step: (0, 0)),
            pl.BlockSpec(shared_up.shape, lambda step: (0, 0)),
            pl.BlockSpec(shared_down.shape, lambda step: (0, 0)),
        ],
        out_specs=pl.BlockSpec((count, width), lambda step: (0, 0)),
        out_shape=jax.ShapeDtypeStruct((count, width), jnp.bfloat16),
        scratch_shapes=[pltpu.VMEM((count, width), jnp.float32)],
        cost_estimate=pl.CostEstimate(
            flops=6 * count * width * (pieces * units + shared_gate.shape[0]),
            transcendentals=count * (pieces * units + shared_gate.shape[0]),
            bytes_accessed=weight_bytes + 4 * count * width,
        ),
    )(rows, weight_table, gate_pieces, up_pieces, down_pieces, shared_gate, shared_up, shared_down)


def on_device(
    token_ids,
    cache_lengths,
    empty_blocks,
    expert_ids,
    embed_table,
    attn_gain,
    w_query,
    w_key,
    w_value,
    w_out,
    k_cache,
    v_cache,
    moe_gain,
    w_router,
    gate_pieces,
    up_pieces,
    down_pieces,
    shared_gate,
    shared_up,
    shared_down,
    final_gain,
    w_head,
):
    steps, requests = token_ids.shape
    tokens = steps * requests
    width = embed_table.shape[1]
    vocab_local = embed_table.shape[0]
    n_seq = lax.axis_size("seq")
    n_exp = lax.axis_size("exp")
    n_dev = n_seq * n_exp
    owner_index = lax.axis_index(("seq", "exp"))
    seq_index = lax.axis_index("seq")
    own_count = requests // n_exp
    own_start = lax.axis_index("exp") * own_count
    group = steps * own_count
    share = group // n_seq

    def grouped(values):
        rest = values.shape[2:]
        by_group = jnp.moveaxis(values.reshape((steps, n_exp, own_count) + rest), 1, 0)
        return by_group.reshape((tokens,) + rest)


    def natural(values):
        split = jnp.swapaxes(values.reshape(n_seq, n_exp, share), 0, 1)
        grouped = split.reshape(n_exp, steps, own_count)
        return jnp.moveaxis(grouped, 0, 1).reshape(steps, requests)

    group_ids = jnp.moveaxis(token_ids.reshape(steps, n_exp, own_count), 1, 0)
    local_ids = group_ids - owner_index * vocab_local
    held = (local_ids >= 0) & (local_ids < vocab_local)
    rows = jnp.take(embed_table, jnp.clip(local_ids, 0, vocab_local - 1), axis=0)
    rows = jnp.where(held[..., None], rows, jnp.zeros((), rows.dtype))
    arrived = lax.all_to_all(rows, "exp", 0, 0, tiled=True)
    row_part = jnp.sum(arrived.astype(jnp.float32), axis=0).astype(jnp.bfloat16)
    row_parts = lax.all_gather(row_part, "seq", axis=0, tiled=False)
    embedded = jnp.sum(row_parts.astype(jnp.float32), axis=0).reshape(group, width)

    attn_in = rms_scale(embedded, attn_gain).astype(jnp.bfloat16)
    own_lengths = lax.dynamic_slice_in_dim(cache_lengths, own_start, own_count, 0)
    places = (own_lengths[None, :] + jnp.arange(steps, dtype=jnp.int32)[:, None]).reshape(group)
    heads_here = w_query.shape[1] // HDIM

    def project(weight):
        return jnp.dot(attn_in, weight, preferred_element_type=jnp.float32).reshape(
            group, heads_here, HDIM
        )

    query_part = rotate(project(w_query), places).astype(jnp.bfloat16)
    key_part = rotate(project(w_key), places).astype(jnp.bfloat16)
    value_part = project(w_value).astype(jnp.bfloat16)
    every = lax.all_gather(
        jnp.stack([query_part, key_part, value_part], axis=0), "seq", axis=0, tiled=False
    )
    head_count = n_seq * heads_here
    every = jnp.moveaxis(every, 0, 2).reshape(3, steps, own_count, head_count, HDIM)
    queries = every[0]

    span = k_cache.shape[1]
    first_place = seq_index * span
    places_here = first_place + jnp.arange(span, dtype=jnp.int32)
    own_empty = lax.dynamic_slice_in_dim(empty_blocks, own_start, own_count, 0)
    local_blocks = lax.dynamic_slice_in_dim(own_empty, first_place // BLK, span // BLK, 1)
    blocked = jnp.broadcast_to(local_blocks[:, :, None], (own_count, span // BLK, BLK)).reshape(
        own_count, span
    )
    live_mask = ((places_here[None, :] < own_lengths[:, None]) & (blocked == 0))[None, :, None, :]
    cache_keys = k_cache.reshape(own_count, span, head_count, HDIM)
    cache_values = v_cache.reshape(own_count, span, head_count, HDIM)
    score_scale = 1.0 / math.sqrt(HDIM)
    cached = (
        jnp.einsum("trhd,rphd->trhp", queries, cache_keys, preferred_element_type=jnp.float32)
        * score_scale
    )
    local_top = jnp.max(jnp.where(live_mask, cached, negative), axis=3)
    local_weights = jnp.where(live_mask, jnp.exp(cached - local_top[..., None]), 0.0)
    local_totals = jnp.sum(local_weights, axis=3)
    local_mixture = jnp.einsum(
        "trhp,rphd->trhd",
        local_weights.astype(jnp.bfloat16),
        cache_values,
        preferred_element_type=jnp.float32,
    )

    def by_owner(values):
        rest = values.shape[3:]
        split = values.reshape((steps, own_count, n_seq, heads_here) + rest)
        return jnp.moveaxis(split, 2, 0).reshape(n_seq, -1)

    mix_len = group * heads_here * HDIM
    stat_len = group * heads_here
    packed = jnp.concatenate(
        [by_owner(local_mixture), by_owner(local_top), by_owner(local_totals)], axis=1
    )
    got = lax.all_to_all(packed, "seq", 0, 0, tiled=True)
    got_mixture = got[:, :mix_len].reshape(n_seq, steps, own_count, heads_here, HDIM)
    got_top = got[:, mix_len : mix_len + stat_len].reshape(n_seq, steps, own_count, heads_here)
    got_totals = got[:, mix_len + stat_len :].reshape(n_seq, steps, own_count, heads_here)

    own_queries = query_part.reshape(steps, own_count, heads_here, HDIM)
    own_keys = key_part.reshape(steps, own_count, heads_here, HDIM)
    own_values = value_part.reshape(steps, own_count, heads_here, HDIM)
    fresh_scores = (
        jnp.einsum("trhd,urhd->trhu", own_queries, own_keys, preferred_element_type=jnp.float32)
        * score_scale
    )
    causal = (jnp.arange(steps)[None, :] <= jnp.arange(steps)[:, None])[:, None, None, :]
    fresh_top = jnp.max(jnp.where(causal, fresh_scores, negative), axis=3)
    fresh_weights = jnp.where(causal, jnp.exp(fresh_scores - fresh_top[..., None]), 0.0)
    fresh_mixture = jnp.einsum(
        "trhu,urhd->trhd",
        fresh_weights.astype(jnp.bfloat16),
        own_values,
        preferred_element_type=jnp.float32,
    )
    top_score = jnp.maximum(jnp.max(got_top, axis=0), fresh_top)
    cache_factor = jnp.exp(got_top - top_score[None])
    fresh_factor = jnp.exp(fresh_top - top_score)
    totals = jnp.sum(got_totals * cache_factor, axis=0) + jnp.sum(fresh_weights, axis=3) * fresh_factor
    mixture = (
        jnp.sum(got_mixture * cache_factor[..., None], axis=0)
        + fresh_mixture * fresh_factor[..., None]
    )
    own_heads = (mixture / totals[..., None]).astype(jnp.bfloat16).reshape(
        group, heads_here * HDIM
    )

    attn_part = jnp.dot(own_heads, w_out, preferred_element_type=jnp.float32)
    attn_parts = lax.all_gather(attn_part.astype(jnp.bfloat16), "seq", axis=0, tiled=False)
    resid_group = embedded + jnp.sum(attn_parts.astype(jnp.float32), axis=0)
    resid_share = lax.dynamic_slice_in_dim(resid_group, seq_index * share, share, 0)
    moe_in = lax.all_gather(
        rms_scale(resid_group, moe_gain).astype(jnp.bfloat16), "exp", axis=0, tiled=True
    )

    router = jax.nn.sigmoid(jnp.dot(moe_in, w_router, preferred_element_type=jnp.float32))
    expert_count = w_router.shape[1]
    chosen_ids = grouped(expert_ids)
    picked = chosen_ids[:, :, None] == jnp.arange(expert_count, dtype=jnp.int32)[None, None, :]
    chosen = jnp.sum(jnp.where(picked, router[:, None, :], 0.0), axis=2)
    gate_weights = chosen / jnp.sum(chosen, axis=1, keepdims=True)
    rows_here = gate_pieces.shape[0]
    row_expert = (owner_index * rows_here + jnp.arange(rows_here, dtype=jnp.int32)) // PIECES
    token_weight = jnp.sum(
        jnp.where(
            chosen_ids[:, :, None] == row_expert[None, None, :], gate_weights[:, :, None], 0.0
        ),
        axis=1,
    )
    share_count = tokens // n_seq
    share_start = seq_index * share_count
    token_place = jnp.arange(tokens, dtype=jnp.int32)
    shared_mask = (
        (token_place >= share_start) & (token_place < share_start + share_count)
    ).astype(jnp.float32)[:, None]
    lanes = -(-(rows_here + 1) // 128) * 128
    weight_table = jnp.pad(
        jnp.concatenate([token_weight, shared_mask], axis=1), ((0, 0), (0, lanes - rows_here - 1))
    )
    term_rows = experts(
        moe_in, weight_table, gate_pieces, up_pieces, down_pieces,
        shared_gate, shared_up, shared_down,
    )

    term_sum = jnp.sum(
        lax.all_to_all(
            term_rows.reshape(n_dev, share, width),
            ("exp", "seq"),
            0,
            0,
            tiled=True,
        ).astype(jnp.float32),
        axis=0,
    )
    final_share = resid_share + term_sum
    norms_share = jnp.sqrt(jnp.mean(final_share * final_share, axis=-1))
    head_share = rms_scale(final_share, final_gain).astype(jnp.bfloat16)
    rounds = n_exp.bit_length() - 1
    if n_exp == 1 << rounds:
        for level in reversed(range(rounds)):
            partner = [(i, i ^ (1 << level)) for i in range(n_exp)]
            head_share = jnp.concatenate([head_share, lax.ppermute(head_share, "exp", partner)], 0)
        head_in = lax.all_gather(head_share, "seq", axis=0, tiled=False).reshape(tokens, width)
        local_best = jnp.max(jnp.dot(head_in, w_head, preferred_element_type=jnp.float32), axis=-1)
        flipped = jnp.arange(n_exp, dtype=jnp.int32) ^ lax.axis_index("exp")
        block = sum(((flipped >> bit) & 1) << (rounds - 1 - bit) for bit in range(rounds))
        local_best = jnp.take(local_best.reshape(n_seq, n_exp, share), block, axis=1).reshape(tokens)
    else:
        head_in = gather_all(head_share).reshape(tokens, width)
        local_best = jnp.max(jnp.dot(head_in, w_head, preferred_element_type=jnp.float32), axis=-1)
    message = jnp.concatenate([local_best, norms_share], axis=0)
    heard = lax.all_to_all(
        jnp.broadcast_to(message[None, :], (n_dev, message.shape[0])),
        ("seq", "exp"),
        0,
        0,
        tiled=True,
    )
    greatest_logits = natural(jnp.max(heard[:, :tokens], axis=0))
    hidden_norms = natural(heard[:, tokens:].reshape(tokens))
    return (hidden_norms, greatest_logits)


def solution(mesh):
    in_specs = (
        P(),
        P(),
        P(),
        P(),
        P(("seq", "exp"), None),
        P(),
        P(None, "seq"),
        P(None, "seq"),
        P(None, "seq"),
        P("seq", None),
        P("exp", "seq", None),
        P("exp", "seq", None),
        P(),
        P(),
        P(("seq", "exp"), None, None),
        P(("seq", "exp"), None, None),
        P(("seq", "exp"), None, None),
        P(None, "exp"),
        P(None, "exp"),
        P("exp", None),
        P(),
        P(None, ("seq", "exp")),
    )
    out_specs = (P(), P())
    return jax.shard_map(
        on_device, mesh=mesh, in_specs=in_specs, out_specs=out_specs, check_vma=False
    )
```

```python
import math

import jax
import jax.numpy as jnp
from jax import lax
from jax.experimental import pallas as pl
from jax.experimental.pallas import tpu as pltpu
from jax.sharding import PartitionSpec as P

HDIM = 128
PIECES = 4
BLK = 16


epsilon = 1e-06
negative = -1e30


def rms_scale(values, scales):
    return values * lax.rsqrt(jnp.mean(values * values, axis=-1, keepdims=True) + epsilon) * scales


def rotate(values, places):
    half_width = values.shape[-1] // 2
    frequency = 10000.0 ** (-2.0 * jnp.arange(half_width, dtype=jnp.float32) / values.shape[-1])
    angles = places.astype(jnp.float32)[..., None, None] * frequency
    cosine_table = jnp.cos(angles)
    sine_table = jnp.sin(angles)
    lower = values[..., :half_width]
    upper = values[..., half_width:]
    return jnp.concatenate(
        [lower * cosine_table - upper * sine_table, upper * cosine_table + lower * sine_table],
        axis=-1,
    )


def gather_all(values):
    inner = lax.all_gather(values, "exp", axis=0, tiled=False)
    return lax.all_gather(inner, "seq", axis=0, tiled=False)


def experts_kernel(pieces, x_ref, weight_ref, gate_ref, up_ref, down_ref, sgate_ref, sup_ref, sdown_ref, out_ref, total_ref):
    step = pl.program_id(0)

    @pl.when(step == 0)
    def _():
        total_ref[...] = jnp.zeros_like(total_ref)

    def one_piece(gate, up, down, scale):
        rows = x_ref[...]
        along = (((1,), (1,)), ((), ()))
        gate_out = lax.dot_general(rows, gate, along, preferred_element_type=jnp.float32)
        up_out = lax.dot_general(rows, up, along, preferred_element_type=jnp.float32)
        hidden = (gate_out * jax.nn.sigmoid(gate_out) * up_out * scale).astype(jnp.bfloat16)
        total_ref[...] += jnp.dot(hidden, down, preferred_element_type=jnp.float32)

    table = weight_ref[...]
    column = lax.broadcasted_iota(jnp.int32, table.shape, 1)
    scale = jnp.sum(jnp.where(column == step, table, 0.0), axis=1, keepdims=True)

    @pl.when(step < pieces)
    def _():
        one_piece(gate_ref[0], up_ref[0], down_ref[0], scale)

    @pl.when(step == pieces)
    def _():
        one_piece(sgate_ref[...], sup_ref[...], sdown_ref[...], scale)
        out_ref[...] = total_ref[...].astype(out_ref.dtype)


def experts(rows, weight_table, gate_pieces, up_pieces, down_pieces, shared_gate, shared_up, shared_down):
    gate_pieces = jnp.swapaxes(gate_pieces, 1, 2)
    up_pieces = jnp.swapaxes(up_pieces, 1, 2)
    shared_gate = shared_gate.T
    shared_up = shared_up.T
    pieces, units, width = gate_pieces.shape
    count = rows.shape[0]
    last = pieces - 1

    def piece_map(step):
        return (jnp.minimum(step, last), 0, 0)

    weight_bytes = 2 * 3 * width * (pieces * units + shared_gate.shape[0])
    return pl.pallas_call(
        lambda *refs: experts_kernel(pieces, *refs),
        grid=(pieces + 1,),
        in_specs=[
            pl.BlockSpec((count, width), lambda step: (0, 0)),
            pl.BlockSpec(weight_table.shape, lambda step: (0, 0)),
            pl.BlockSpec((1, units, width), piece_map),
            pl.BlockSpec((1, units, width), piece_map),
            pl.BlockSpec((1, units, width), piece_map),
            pl.BlockSpec(shared_gate.shape, lambda step: (0, 0)),
            pl.BlockSpec(shared_up.shape, lambda step: (0, 0)),
            pl.BlockSpec(shared_down.shape, lambda step: (0, 0)),
        ],
        out_specs=pl.BlockSpec((count, width), lambda step: (0, 0)),
        out_shape=jax.ShapeDtypeStruct((count, width), jnp.bfloat16),
        scratch_shapes=[pltpu.VMEM((count, width), jnp.float32)],
        cost_estimate=pl.CostEstimate(
            flops=6 * count * width * (pieces * units + shared_gate.shape[0]),
            transcendentals=count * (pieces * units + shared_gate.shape[0]),
            bytes_accessed=weight_bytes + 4 * count * width,
        ),
    )(rows, weight_table, gate_pieces, up_pieces, down_pieces, shared_gate, shared_up, shared_down)


def on_device(
    token_ids,
    cache_lengths,
    empty_blocks,
    expert_ids,
    embed_table,
    attn_gain,
    w_query,
    w_key,
    w_value,
    w_out,
    k_cache,
    v_cache,
    moe_gain,
    w_router,
    gate_pieces,
    up_pieces,
    down_pieces,
    shared_gate,
    shared_up,
    shared_down,
    final_gain,
    w_head,
):
    steps, requests = token_ids.shape
    tokens = steps * requests
    width = embed_table.shape[1]
    vocab_local = embed_table.shape[0]
    n_seq = lax.axis_size("seq")
    n_exp = lax.axis_size("exp")
    n_dev = n_seq * n_exp
    owner_index = lax.axis_index(("seq", "exp"))
    seq_index = lax.axis_index("seq")
    own_count = requests // n_exp
    own_start = lax.axis_index("exp") * own_count
    group = steps * own_count
    share = group // n_seq

    def grouped(values):
        rest = values.shape[2:]
        by_group = jnp.moveaxis(values.reshape((steps, n_exp, own_count) + rest), 1, 0)
        return by_group.reshape((tokens,) + rest)


    def natural(values):
        split = jnp.swapaxes(values.reshape(n_seq, n_exp, share), 0, 1)
        grouped = split.reshape(n_exp, steps, own_count)
        return jnp.moveaxis(grouped, 0, 1).reshape(steps, requests)

    group_ids = jnp.moveaxis(token_ids.reshape(steps, n_exp, own_count), 1, 0)
    local_ids = group_ids - owner_index * vocab_local
    held = (local_ids >= 0) & (local_ids < vocab_local)
    rows = jnp.take(embed_table, jnp.clip(local_ids, 0, vocab_local - 1), axis=0)
    rows = jnp.where(held[..., None], rows, jnp.zeros((), rows.dtype))
    arrived = lax.all_to_all(rows, "exp", 0, 0, tiled=True)
    row_part = jnp.sum(arrived.astype(jnp.float32), axis=0).astype(jnp.bfloat16)
    row_parts = lax.all_gather(row_part, "seq", axis=0, tiled=False)
    embedded = jnp.sum(row_parts.astype(jnp.float32), axis=0).reshape(group, width)

    attn_in = rms_scale(embedded, attn_gain).astype(jnp.bfloat16)
    own_lengths = lax.dynamic_slice_in_dim(cache_lengths, own_start, own_count, 0)
    places = (own_lengths[None, :] + jnp.arange(steps, dtype=jnp.int32)[:, None]).reshape(group)
    heads_here = w_query.shape[1] // HDIM

    def project(weight):
        return jnp.dot(attn_in, weight, preferred_element_type=jnp.float32).reshape(
            group, heads_here, HDIM
        )

    query_part = rotate(project(w_query), places).astype(jnp.bfloat16)
    key_part = rotate(project(w_key), places).astype(jnp.bfloat16)
    value_part = project(w_value).astype(jnp.bfloat16)
    every = lax.all_gather(
        jnp.stack([query_part, key_part, value_part], axis=0), "seq", axis=0, tiled=False
    )
    head_count = n_seq * heads_here
    every = jnp.moveaxis(every, 0, 2).reshape(3, steps, own_count, head_count, HDIM)
    queries = every[0]

    span = k_cache.shape[1]
    first_place = seq_index * span
    places_here = first_place + jnp.arange(span, dtype=jnp.int32)
    own_empty = lax.dynamic_slice_in_dim(empty_blocks, own_start, own_count, 0)
    local_blocks = lax.dynamic_slice_in_dim(own_empty, first_place // BLK, span // BLK, 1)
    blocked = jnp.broadcast_to(local_blocks[:, :, None], (own_count, span // BLK, BLK)).reshape(
        own_count, span
    )
    live_mask = ((places_here[None, :] < own_lengths[:, None]) & (blocked == 0))[None, :, None, :]
    cache_keys = k_cache.reshape(own_count, span, head_count, HDIM)
    cache_values = v_cache.reshape(own_count, span, head_count, HDIM)
    score_scale = 1.0 / math.sqrt(HDIM)
    cached = (
        jnp.einsum("trhd,rphd->trhp", queries, cache_keys, preferred_element_type=jnp.float32)
        * score_scale
    )
    local_top = jnp.max(jnp.where(live_mask, cached, negative), axis=3)
    local_weights = jnp.where(live_mask, jnp.exp(cached - local_top[..., None]), 0.0)
    local_totals = jnp.sum(local_weights, axis=3)
    local_mixture = jnp.einsum(
        "trhp,rphd->trhd",
        local_weights.astype(jnp.bfloat16),
        cache_values,
        preferred_element_type=jnp.float32,
    )

    def by_owner(values):
        rest = values.shape[3:]
        split = values.reshape((steps, own_count, n_seq, heads_here) + rest)
        return jnp.moveaxis(split, 2, 0).reshape(n_seq, -1)

    mix_len = group * heads_here * HDIM
    stat_len = group * heads_here
    packed = jnp.concatenate(
        [by_owner(local_mixture), by_owner(local_top), by_owner(local_totals)], axis=1
    )
    got = lax.all_to_all(packed, "seq", 0, 0, tiled=True)
    got_mixture = got[:, :mix_len].reshape(n_seq, steps, own_count, heads_here, HDIM)
    got_top = got[:, mix_len : mix_len + stat_len].reshape(n_seq, steps, own_count, heads_here)
    got_totals = got[:, mix_len + stat_len :].reshape(n_seq, steps, own_count, heads_here)

    own_queries = query_part.reshape(steps, own_count, heads_here, HDIM)
    own_keys = key_part.reshape(steps, own_count, heads_here, HDIM)
    own_values = value_part.reshape(steps, own_count, heads_here, HDIM)
    fresh_scores = (
        jnp.einsum("trhd,urhd->trhu", own_queries, own_keys, preferred_element_type=jnp.float32)
        * score_scale
    )
    causal = (jnp.arange(steps)[None, :] <= jnp.arange(steps)[:, None])[:, None, None, :]
    fresh_top = jnp.max(jnp.where(causal, fresh_scores, negative), axis=3)
    fresh_weights = jnp.where(causal, jnp.exp(fresh_scores - fresh_top[..., None]), 0.0)
    fresh_mixture = jnp.einsum(
        "trhu,urhd->trhd",
        fresh_weights.astype(jnp.bfloat16),
        own_values,
        preferred_element_type=jnp.float32,
    )
    top_score = jnp.maximum(jnp.max(got_top, axis=0), fresh_top)
    cache_factor = jnp.exp(got_top - top_score[None])
    fresh_factor = jnp.exp(fresh_top - top_score)
    totals = jnp.sum(got_totals * cache_factor, axis=0) + jnp.sum(fresh_weights, axis=3) * fresh_factor
    mixture = (
        jnp.sum(got_mixture * cache_factor[..., None], axis=0)
        + fresh_mixture * fresh_factor[..., None]
    )
    own_heads = (mixture / totals[..., None]).astype(jnp.bfloat16).reshape(
        group, heads_here * HDIM
    )

    attn_part = jnp.dot(own_heads, w_out, preferred_element_type=jnp.float32)
    attn_parts = lax.all_gather(attn_part.astype(jnp.bfloat16), "seq", axis=0, tiled=False)
    resid_group = embedded + jnp.sum(attn_parts.astype(jnp.float32), axis=0)
    resid_share = lax.dynamic_slice_in_dim(resid_group, seq_index * share, share, 0)
    moe_group = rms_scale(resid_group, moe_gain).astype(jnp.bfloat16)
    rounds = n_exp.bit_length() - 1
    if n_exp == 1 << rounds:
        flipped = jnp.arange(n_exp, dtype=jnp.int32) ^ lax.axis_index("exp")
        block = sum(((flipped >> bit) & 1) << (rounds - 1 - bit) for bit in range(rounds))
        for level in reversed(range(rounds)):
            partner = [(i, i ^ (1 << level)) for i in range(n_exp)]
            moe_group = jnp.concatenate([moe_group, lax.ppermute(moe_group, "exp", partner)], 0)
        moe_in = jnp.take(moe_group.reshape(n_exp, group, width), block, axis=0).reshape(
            tokens, width
        )
    else:
        moe_in = lax.all_gather(moe_group, "exp", axis=0, tiled=True)

    router = jax.nn.sigmoid(jnp.dot(moe_in, w_router, preferred_element_type=jnp.float32))
    expert_count = w_router.shape[1]
    chosen_ids = grouped(expert_ids)
    picked = chosen_ids[:, :, None] == jnp.arange(expert_count, dtype=jnp.int32)[None, None, :]
    chosen = jnp.sum(jnp.where(picked, router[:, None, :], 0.0), axis=2)
    gate_weights = chosen / jnp.sum(chosen, axis=1, keepdims=True)
    rows_here = gate_pieces.shape[0]
    row_expert = (owner_index * rows_here + jnp.arange(rows_here, dtype=jnp.int32)) // PIECES
    token_weight = jnp.sum(
        jnp.where(
            chosen_ids[:, :, None] == row_expert[None, None, :], gate_weights[:, :, None], 0.0
        ),
        axis=1,
    )
    share_count = tokens // n_seq
    share_start = seq_index * share_count
    token_place = jnp.arange(tokens, dtype=jnp.int32)
    shared_mask = (
        (token_place >= share_start) & (token_place < share_start + share_count)
    ).astype(jnp.float32)[:, None]
    lanes = -(-(rows_here + 1) // 128) * 128
    weight_table = jnp.pad(
        jnp.concatenate([token_weight, shared_mask], axis=1), ((0, 0), (0, lanes - rows_here - 1))
    )
    term_rows = experts(
        moe_in, weight_table, gate_pieces, up_pieces, down_pieces,
        shared_gate, shared_up, shared_down,
    )

    term_sum = jnp.sum(
        lax.all_to_all(
            term_rows.reshape(n_dev, share, width),
            ("exp", "seq"),
            0,
            0,
            tiled=True,
        ).astype(jnp.float32),
        axis=0,
    )
    final_share = resid_share + term_sum
    norms_share = jnp.sqrt(jnp.mean(final_share * final_share, axis=-1))
    head_share = rms_scale(final_share, final_gain).astype(jnp.bfloat16)
    if n_exp == 1 << rounds:
        for level in reversed(range(rounds)):
            partner = [(i, i ^ (1 << level)) for i in range(n_exp)]
            head_share = jnp.concatenate([head_share, lax.ppermute(head_share, "exp", partner)], 0)
        head_in = lax.all_gather(head_share, "seq", axis=0, tiled=False).reshape(tokens, width)
        local_best = jnp.max(jnp.dot(head_in, w_head, preferred_element_type=jnp.float32), axis=-1)
        local_best = jnp.take(local_best.reshape(n_seq, n_exp, share), block, axis=1).reshape(tokens)
    else:
        head_in = gather_all(head_share).reshape(tokens, width)
        local_best = jnp.max(jnp.dot(head_in, w_head, preferred_element_type=jnp.float32), axis=-1)
    message = jnp.concatenate([local_best, norms_share], axis=0)
    heard = lax.all_to_all(
        jnp.broadcast_to(message[None, :], (n_dev, message.shape[0])),
        ("seq", "exp"),
        0,
        0,
        tiled=True,
    )
    greatest_logits = natural(jnp.max(heard[:, :tokens], axis=0))
    hidden_norms = natural(heard[:, tokens:].reshape(tokens))
    return (hidden_norms, greatest_logits)


def solution(mesh):
    in_specs = (
        P(),
        P(),
        P(),
        P(),
        P(("seq", "exp"), None),
        P(),
        P(None, "seq"),
        P(None, "seq"),
        P(None, "seq"),
        P("seq", None),
        P("exp", "seq", None),
        P("exp", "seq", None),
        P(),
        P(),
        P(("seq", "exp"), None, None),
        P(("seq", "exp"), None, None),
        P(("seq", "exp"), None, None),
        P(None, "exp"),
        P(None, "exp"),
        P("exp", None),
        P(),
        P(None, ("seq", "exp")),
    )
    out_specs = (P(), P())
    return jax.shard_map(
        on_device, mesh=mesh, in_specs=in_specs, out_specs=out_specs, check_vma=False
    )
```

```python
import math

import jax
import jax.numpy as jnp
from jax import lax
from jax.experimental import pallas as pl
from jax.experimental.pallas import tpu as pltpu
from jax.sharding import PartitionSpec as P

HDIM = 128
PIECES = 4
BLK = 16


epsilon = 1e-06
negative = -1e30


def rms_scale(values, scales):
    return values * lax.rsqrt(jnp.mean(values * values, axis=-1, keepdims=True) + epsilon) * scales


def rotate(values, places):
    half_width = values.shape[-1] // 2
    frequency = 10000.0 ** (-2.0 * jnp.arange(half_width, dtype=jnp.float32) / values.shape[-1])
    angles = places.astype(jnp.float32)[..., None, None] * frequency
    cosine_table = jnp.cos(angles)
    sine_table = jnp.sin(angles)
    lower = values[..., :half_width]
    upper = values[..., half_width:]
    return jnp.concatenate(
        [lower * cosine_table - upper * sine_table, upper * cosine_table + lower * sine_table],
        axis=-1,
    )


def gather_all(values):
    inner = lax.all_gather(values, "exp", axis=0, tiled=False)
    return lax.all_gather(inner, "seq", axis=0, tiled=False)


def butterfly(values, axis, count):
    rounds = count.bit_length() - 1
    stacked = values[None]
    for level in reversed(range(rounds)):
        partner = [(i, i ^ (1 << level)) for i in range(count)]
        stacked = jnp.concatenate([stacked, lax.ppermute(stacked, axis, partner)], 0)
    flipped = jnp.arange(count, dtype=jnp.int32) ^ lax.axis_index(axis)
    block = sum(((flipped >> bit) & 1) << (rounds - 1 - bit) for bit in range(rounds))
    return stacked, block


def gather_seq(values, ordered):
    count = lax.axis_size("seq")
    if count != 1 << (count.bit_length() - 1):
        return lax.all_gather(values, "seq", axis=0, tiled=False)
    stacked, block = butterfly(values, "seq", count)
    return jnp.take(stacked, block, axis=0) if ordered else stacked


def experts_kernel(pieces, x_ref, weight_ref, gate_ref, up_ref, down_ref, sgate_ref, sup_ref, sdown_ref, out_ref, total_ref):
    step = pl.program_id(0)

    @pl.when(step == 0)
    def _():
        total_ref[...] = jnp.zeros_like(total_ref)

    def one_piece(gate, up, down, scale):
        rows = x_ref[...]
        along = (((1,), (1,)), ((), ()))
        gate_out = lax.dot_general(rows, gate, along, preferred_element_type=jnp.float32)
        up_out = lax.dot_general(rows, up, along, preferred_element_type=jnp.float32)
        hidden = (gate_out * jax.nn.sigmoid(gate_out) * up_out * scale).astype(jnp.bfloat16)
        total_ref[...] += jnp.dot(hidden, down, preferred_element_type=jnp.float32)

    table = weight_ref[...]
    column = lax.broadcasted_iota(jnp.int32, table.shape, 1)
    scale = jnp.sum(jnp.where(column == step, table, 0.0), axis=1, keepdims=True)

    @pl.when(step < pieces)
    def _():
        one_piece(gate_ref[0], up_ref[0], down_ref[0], scale)

    @pl.when(step == pieces)
    def _():
        one_piece(sgate_ref[...], sup_ref[...], sdown_ref[...], scale)
        out_ref[...] = total_ref[...].astype(out_ref.dtype)


def experts(rows, weight_table, gate_pieces, up_pieces, down_pieces, shared_gate, shared_up, shared_down):
    gate_pieces = jnp.swapaxes(gate_pieces, 1, 2)
    up_pieces = jnp.swapaxes(up_pieces, 1, 2)
    shared_gate = shared_gate.T
    shared_up = shared_up.T
    pieces, units, width = gate_pieces.shape
    count = rows.shape[0]
    last = pieces - 1

    def piece_map(step):
        return (jnp.minimum(step, last), 0, 0)

    weight_bytes = 2 * 3 * width * (pieces * units + shared_gate.shape[0])
    return pl.pallas_call(
        lambda *refs: experts_kernel(pieces, *refs),
        grid=(pieces + 1,),
        in_specs=[
            pl.BlockSpec((count, width), lambda step: (0, 0)),
            pl.BlockSpec(weight_table.shape, lambda step: (0, 0)),
            pl.BlockSpec((1, units, width), piece_map),
            pl.BlockSpec((1, units, width), piece_map),
            pl.BlockSpec((1, units, width), piece_map),
            pl.BlockSpec(shared_gate.shape, lambda step: (0, 0)),
            pl.BlockSpec(shared_up.shape, lambda step: (0, 0)),
            pl.BlockSpec(shared_down.shape, lambda step: (0, 0)),
        ],
        out_specs=pl.BlockSpec((count, width), lambda step: (0, 0)),
        out_shape=jax.ShapeDtypeStruct((count, width), jnp.bfloat16),
        scratch_shapes=[pltpu.VMEM((count, width), jnp.float32)],
        cost_estimate=pl.CostEstimate(
            flops=6 * count * width * (pieces * units + shared_gate.shape[0]),
            transcendentals=count * (pieces * units + shared_gate.shape[0]),
            bytes_accessed=weight_bytes + 4 * count * width,
        ),
    )(rows, weight_table, gate_pieces, up_pieces, down_pieces, shared_gate, shared_up, shared_down)


def on_device(
    token_ids,
    cache_lengths,
    empty_blocks,
    expert_ids,
    embed_table,
    attn_gain,
    w_query,
    w_key,
    w_value,
    w_out,
    k_cache,
    v_cache,
    moe_gain,
    w_router,
    gate_pieces,
    up_pieces,
    down_pieces,
    shared_gate,
    shared_up,
    shared_down,
    final_gain,
    w_head,
):
    steps, requests = token_ids.shape
    tokens = steps * requests
    width = embed_table.shape[1]
    vocab_local = embed_table.shape[0]
    n_seq = lax.axis_size("seq")
    n_exp = lax.axis_size("exp")
    n_dev = n_seq * n_exp
    owner_index = lax.axis_index(("seq", "exp"))
    seq_index = lax.axis_index("seq")
    own_count = requests // n_exp
    own_start = lax.axis_index("exp") * own_count
    group = steps * own_count
    share = group // n_seq

    def grouped(values):
        rest = values.shape[2:]
        by_group = jnp.moveaxis(values.reshape((steps, n_exp, own_count) + rest), 1, 0)
        return by_group.reshape((tokens,) + rest)


    def natural(values):
        split = jnp.swapaxes(values.reshape(n_seq, n_exp, share), 0, 1)
        grouped = split.reshape(n_exp, steps, own_count)
        return jnp.moveaxis(grouped, 0, 1).reshape(steps, requests)

    group_ids = jnp.moveaxis(token_ids.reshape(steps, n_exp, own_count), 1, 0)
    local_ids = group_ids - owner_index * vocab_local
    held = (local_ids >= 0) & (local_ids < vocab_local)
    rows = jnp.take(embed_table, jnp.clip(local_ids, 0, vocab_local - 1), axis=0)
    rows = jnp.where(held[..., None], rows, jnp.zeros((), rows.dtype))
    arrived = lax.all_to_all(rows, "exp", 0, 0, tiled=True)
    row_part = jnp.sum(arrived.astype(jnp.float32), axis=0).astype(jnp.bfloat16)
    row_parts = gather_seq(row_part, False)
    embedded = jnp.sum(row_parts.astype(jnp.float32), axis=0).reshape(group, width)

    attn_in = rms_scale(embedded, attn_gain).astype(jnp.bfloat16)
    own_lengths = lax.dynamic_slice_in_dim(cache_lengths, own_start, own_count, 0)
    places = (own_lengths[None, :] + jnp.arange(steps, dtype=jnp.int32)[:, None]).reshape(group)
    heads_here = w_query.shape[1] // HDIM

    def project(weight):
        return jnp.dot(attn_in, weight, preferred_element_type=jnp.float32).reshape(
            group, heads_here, HDIM
        )

    query_part = rotate(project(w_query), places).astype(jnp.bfloat16)
    key_part = rotate(project(w_key), places).astype(jnp.bfloat16)
    value_part = project(w_value).astype(jnp.bfloat16)
    every = gather_seq(jnp.stack([query_part, key_part, value_part], axis=0), True)
    head_count = n_seq * heads_here
    every = jnp.moveaxis(every, 0, 2).reshape(3, steps, own_count, head_count, HDIM)
    queries = every[0]

    span = k_cache.shape[1]
    first_place = seq_index * span
    places_here = first_place + jnp.arange(span, dtype=jnp.int32)
    own_empty = lax.dynamic_slice_in_dim(empty_blocks, own_start, own_count, 0)
    local_blocks = lax.dynamic_slice_in_dim(own_empty, first_place // BLK, span // BLK, 1)
    blocked = jnp.broadcast_to(local_blocks[:, :, None], (own_count, span // BLK, BLK)).reshape(
        own_count, span
    )
    live_mask = ((places_here[None, :] < own_lengths[:, None]) & (blocked == 0))[None, :, None, :]
    cache_keys = k_cache.reshape(own_count, span, head_count, HDIM)
    cache_values = v_cache.reshape(own_count, span, head_count, HDIM)
    score_scale = 1.0 / math.sqrt(HDIM)
    cached = (
        jnp.einsum("trhd,rphd->trhp", queries, cache_keys, preferred_element_type=jnp.float32)
        * score_scale
    )
    local_top = jnp.max(jnp.where(live_mask, cached, negative), axis=3)
    local_weights = jnp.where(live_mask, jnp.exp(cached - local_top[..., None]), 0.0)
    local_totals = jnp.sum(local_weights, axis=3)
    local_mixture = jnp.einsum(
        "trhp,rphd->trhd",
        local_weights.astype(jnp.bfloat16),
        cache_values,
        preferred_element_type=jnp.float32,
    )

    def by_owner(values):
        rest = values.shape[3:]
        split = values.reshape((steps, own_count, n_seq, heads_here) + rest)
        return jnp.moveaxis(split, 2, 0).reshape(n_seq, -1)

    mix_len = group * heads_here * HDIM
    stat_len = group * heads_here
    packed = jnp.concatenate(
        [by_owner(local_mixture), by_owner(local_top), by_owner(local_totals)], axis=1
    )
    got = lax.all_to_all(packed, "seq", 0, 0, tiled=True)
    got_mixture = got[:, :mix_len].reshape(n_seq, steps, own_count, heads_here, HDIM)
    got_top = got[:, mix_len : mix_len + stat_len].reshape(n_seq, steps, own_count, heads_here)
    got_totals = got[:, mix_len + stat_len :].reshape(n_seq, steps, own_count, heads_here)

    own_queries = query_part.reshape(steps, own_count, heads_here, HDIM)
    own_keys = key_part.reshape(steps, own_count, heads_here, HDIM)
    own_values = value_part.reshape(steps, own_count, heads_here, HDIM)
    fresh_scores = (
        jnp.einsum("trhd,urhd->trhu", own_queries, own_keys, preferred_element_type=jnp.float32)
        * score_scale
    )
    causal = (jnp.arange(steps)[None, :] <= jnp.arange(steps)[:, None])[:, None, None, :]
    fresh_top = jnp.max(jnp.where(causal, fresh_scores, negative), axis=3)
    fresh_weights = jnp.where(causal, jnp.exp(fresh_scores - fresh_top[..., None]), 0.0)
    fresh_mixture = jnp.einsum(
        "trhu,urhd->trhd",
        fresh_weights.astype(jnp.bfloat16),
        own_values,
        preferred_element_type=jnp.float32,
    )
    top_score = jnp.maximum(jnp.max(got_top, axis=0), fresh_top)
    cache_factor = jnp.exp(got_top - top_score[None])
    fresh_factor = jnp.exp(fresh_top - top_score)
    totals = jnp.sum(got_totals * cache_factor, axis=0) + jnp.sum(fresh_weights, axis=3) * fresh_factor
    mixture = (
        jnp.sum(got_mixture * cache_factor[..., None], axis=0)
        + fresh_mixture * fresh_factor[..., None]
    )
    own_heads = (mixture / totals[..., None]).astype(jnp.bfloat16).reshape(
        group, heads_here * HDIM
    )

    attn_part = jnp.dot(own_heads, w_out, preferred_element_type=jnp.float32)
    attn_parts = gather_seq(attn_part.astype(jnp.bfloat16), False)
    resid_group = embedded + jnp.sum(attn_parts.astype(jnp.float32), axis=0)
    resid_share = lax.dynamic_slice_in_dim(resid_group, seq_index * share, share, 0)
    moe_group = rms_scale(resid_group, moe_gain).astype(jnp.bfloat16)
    rounds = n_exp.bit_length() - 1
    if n_exp == 1 << rounds:
        flipped = jnp.arange(n_exp, dtype=jnp.int32) ^ lax.axis_index("exp")
        block = sum(((flipped >> bit) & 1) << (rounds - 1 - bit) for bit in range(rounds))
        for level in reversed(range(rounds)):
            partner = [(i, i ^ (1 << level)) for i in range(n_exp)]
            moe_group = jnp.concatenate([moe_group, lax.ppermute(moe_group, "exp", partner)], 0)
        moe_in = jnp.take(moe_group.reshape(n_exp, group, width), block, axis=0).reshape(
            tokens, width
        )
    else:
        moe_in = lax.all_gather(moe_group, "exp", axis=0, tiled=True)

    router = jax.nn.sigmoid(jnp.dot(moe_in, w_router, preferred_element_type=jnp.float32))
    expert_count = w_router.shape[1]
    chosen_ids = grouped(expert_ids)
    picked = chosen_ids[:, :, None] == jnp.arange(expert_count, dtype=jnp.int32)[None, None, :]
    chosen = jnp.sum(jnp.where(picked, router[:, None, :], 0.0), axis=2)
    gate_weights = chosen / jnp.sum(chosen, axis=1, keepdims=True)
    rows_here = gate_pieces.shape[0]
    row_expert = (owner_index * rows_here + jnp.arange(rows_here, dtype=jnp.int32)) // PIECES
    token_weight = jnp.sum(
        jnp.where(
            chosen_ids[:, :, None] == row_expert[None, None, :], gate_weights[:, :, None], 0.0
        ),
        axis=1,
    )
    share_count = tokens // n_seq
    share_start = seq_index * share_count
    token_place = jnp.arange(tokens, dtype=jnp.int32)
    shared_mask = (
        (token_place >= share_start) & (token_place < share_start + share_count)
    ).astype(jnp.float32)[:, None]
    lanes = -(-(rows_here + 1) // 128) * 128
    weight_table = jnp.pad(
        jnp.concatenate([token_weight, shared_mask], axis=1), ((0, 0), (0, lanes - rows_here - 1))
    )
    term_rows = experts(
        moe_in, weight_table, gate_pieces, up_pieces, down_pieces,
        shared_gate, shared_up, shared_down,
    )

    term_sum = jnp.sum(
        lax.all_to_all(
            term_rows.reshape(n_dev, share, width),
            ("exp", "seq"),
            0,
            0,
            tiled=True,
        ).astype(jnp.float32),
        axis=0,
    )
    final_share = resid_share + term_sum
    norms_share = jnp.sqrt(jnp.mean(final_share * final_share, axis=-1))
    head_share = rms_scale(final_share, final_gain).astype(jnp.bfloat16)
    if n_exp == 1 << rounds:
        for level in reversed(range(rounds)):
            partner = [(i, i ^ (1 << level)) for i in range(n_exp)]
            head_share = jnp.concatenate([head_share, lax.ppermute(head_share, "exp", partner)], 0)
        head_in = lax.all_gather(head_share, "seq", axis=0, tiled=False).reshape(tokens, width)
        local_best = jnp.max(jnp.dot(head_in, w_head, preferred_element_type=jnp.float32), axis=-1)
        local_best = jnp.take(local_best.reshape(n_seq, n_exp, share), block, axis=1).reshape(tokens)
    else:
        head_in = gather_all(head_share).reshape(tokens, width)
        local_best = jnp.max(jnp.dot(head_in, w_head, preferred_element_type=jnp.float32), axis=-1)
    message = jnp.concatenate([local_best, norms_share], axis=0)
    heard = lax.all_to_all(
        jnp.broadcast_to(message[None, :], (n_dev, message.shape[0])),
        ("seq", "exp"),
        0,
        0,
        tiled=True,
    )
    greatest_logits = natural(jnp.max(heard[:, :tokens], axis=0))
    hidden_norms = natural(heard[:, tokens:].reshape(tokens))
    return (hidden_norms, greatest_logits)


def solution(mesh):
    in_specs = (
        P(),
        P(),
        P(),
        P(),
        P(("seq", "exp"), None),
        P(),
        P(None, "seq"),
        P(None, "seq"),
        P(None, "seq"),
        P("seq", None),
        P("exp", "seq", None),
        P("exp", "seq", None),
        P(),
        P(),
        P(("seq", "exp"), None, None),
        P(("seq", "exp"), None, None),
        P(("seq", "exp"), None, None),
        P(None, "exp"),
        P(None, "exp"),
        P("exp", None),
        P(),
        P(None, ("seq", "exp")),
    )
    out_specs = (P(), P())
    return jax.shard_map(
        on_device, mesh=mesh, in_specs=in_specs, out_specs=out_specs, check_vma=False
    )
```

```python
import math

import jax
import jax.numpy as jnp
from jax import lax
from jax.experimental import pallas as pl
from jax.experimental.pallas import tpu as pltpu
from jax.sharding import PartitionSpec as P

HDIM = 128
PIECES = 4
BLK = 16


epsilon = 1e-06
negative = -1e30


def rms_scale(values, scales):
    return values * lax.rsqrt(jnp.mean(values * values, axis=-1, keepdims=True) + epsilon) * scales


def rotate(values, places):
    half_width = values.shape[-1] // 2
    frequency = 10000.0 ** (-2.0 * jnp.arange(half_width, dtype=jnp.float32) / values.shape[-1])
    angles = places.astype(jnp.float32)[..., None, None] * frequency
    cosine_table = jnp.cos(angles)
    sine_table = jnp.sin(angles)
    lower = values[..., :half_width]
    upper = values[..., half_width:]
    return jnp.concatenate(
        [lower * cosine_table - upper * sine_table, upper * cosine_table + lower * sine_table],
        axis=-1,
    )


def gather_all(values):
    inner = lax.all_gather(values, "exp", axis=0, tiled=False)
    return lax.all_gather(inner, "seq", axis=0, tiled=False)


def experts_kernel(pieces, x_ref, weight_ref, gate_ref, up_ref, down_ref, sgate_ref, sup_ref, sdown_ref, out_ref, total_ref):
    step = pl.program_id(0)

    @pl.when(step == 0)
    def _():
        total_ref[...] = jnp.zeros_like(total_ref)

    def one_piece(gate, up, down, scale):
        rows = x_ref[...]
        along = (((1,), (1,)), ((), ()))
        gate_out = lax.dot_general(rows, gate, along, preferred_element_type=jnp.float32)
        up_out = lax.dot_general(rows, up, along, preferred_element_type=jnp.float32)
        hidden = (gate_out * jax.nn.sigmoid(gate_out) * up_out * scale).astype(jnp.bfloat16)
        total_ref[...] += jnp.dot(hidden, down, preferred_element_type=jnp.float32)

    table = weight_ref[...]
    column = lax.broadcasted_iota(jnp.int32, table.shape, 1)
    scale = jnp.sum(jnp.where(column == step, table, 0.0), axis=1, keepdims=True)

    @pl.when(step < pieces)
    def _():
        one_piece(gate_ref[0], up_ref[0], down_ref[0], scale)

    @pl.when(step == pieces)
    def _():
        one_piece(sgate_ref[...], sup_ref[...], sdown_ref[...], scale)
        out_ref[...] = total_ref[...].astype(out_ref.dtype)


def experts(rows, weight_table, gate_pieces, up_pieces, down_pieces, shared_gate, shared_up, shared_down):
    gate_pieces = jnp.swapaxes(gate_pieces, 1, 2)
    up_pieces = jnp.swapaxes(up_pieces, 1, 2)
    shared_gate = shared_gate.T
    shared_up = shared_up.T
    pieces, units, width = gate_pieces.shape
    count = rows.shape[0]
    last = pieces - 1

    def piece_map(step):
        return (jnp.minimum(step, last), 0, 0)

    weight_bytes = 2 * 3 * width * (pieces * units + shared_gate.shape[0])
    return pl.pallas_call(
        lambda *refs: experts_kernel(pieces, *refs),
        grid=(pieces + 1,),
        in_specs=[
            pl.BlockSpec((count, width), lambda step: (0, 0)),
            pl.BlockSpec(weight_table.shape, lambda step: (0, 0)),
            pl.BlockSpec((1, units, width), piece_map),
            pl.BlockSpec((1, units, width), piece_map),
            pl.BlockSpec((1, units, width), piece_map),
            pl.BlockSpec(shared_gate.shape, lambda step: (0, 0)),
            pl.BlockSpec(shared_up.shape, lambda step: (0, 0)),
            pl.BlockSpec(shared_down.shape, lambda step: (0, 0)),
        ],
        out_specs=pl.BlockSpec((count, width), lambda step: (0, 0)),
        out_shape=jax.ShapeDtypeStruct((count, width), jnp.bfloat16),
        scratch_shapes=[pltpu.VMEM((count, width), jnp.float32)],
        cost_estimate=pl.CostEstimate(
            flops=6 * count * width * (pieces * units + shared_gate.shape[0]),
            transcendentals=count * (pieces * units + shared_gate.shape[0]),
            bytes_accessed=weight_bytes + 4 * count * width,
        ),
    )(rows, weight_table, gate_pieces, up_pieces, down_pieces, shared_gate, shared_up, shared_down)


def on_device(
    token_ids,
    cache_lengths,
    empty_blocks,
    expert_ids,
    embed_table,
    attn_gain,
    w_query,
    w_key,
    w_value,
    w_out,
    k_cache,
    v_cache,
    moe_gain,
    w_router,
    gate_pieces,
    up_pieces,
    down_pieces,
    shared_gate,
    shared_up,
    shared_down,
    final_gain,
    w_head,
):
    steps, requests = token_ids.shape
    tokens = steps * requests
    width = embed_table.shape[1]
    vocab_local = embed_table.shape[0]
    n_seq = lax.axis_size("seq")
    n_exp = lax.axis_size("exp")
    n_dev = n_seq * n_exp
    owner_index = lax.axis_index(("seq", "exp"))
    seq_index = lax.axis_index("seq")
    own_count = requests // n_exp
    own_start = lax.axis_index("exp") * own_count
    group = steps * own_count
    share = group // n_seq

    def grouped(values):
        rest = values.shape[2:]
        by_group = jnp.moveaxis(values.reshape((steps, n_exp, own_count) + rest), 1, 0)
        return by_group.reshape((tokens,) + rest)


    def natural(values):
        split = jnp.swapaxes(values.reshape(n_seq, n_exp, share), 0, 1)
        grouped = split.reshape(n_exp, steps, own_count)
        return jnp.moveaxis(grouped, 0, 1).reshape(steps, requests)

    group_ids = jnp.moveaxis(token_ids.reshape(steps, n_exp, own_count), 1, 0)
    local_ids = group_ids - owner_index * vocab_local
    held = (local_ids >= 0) & (local_ids < vocab_local)
    rows = jnp.take(embed_table, jnp.clip(local_ids, 0, vocab_local - 1), axis=0)
    rows = jnp.where(held[..., None], rows, jnp.zeros((), rows.dtype))
    arrived = lax.all_to_all(rows, "exp", 0, 0, tiled=True)
    row_part = jnp.sum(arrived.astype(jnp.float32), axis=0).astype(jnp.bfloat16)
    row_parts = lax.all_gather(row_part, "seq", axis=0, tiled=False)
    embedded = jnp.sum(row_parts.astype(jnp.float32), axis=0).reshape(group, width)

    attn_in = rms_scale(embedded, attn_gain).astype(jnp.bfloat16)
    own_lengths = lax.dynamic_slice_in_dim(cache_lengths, own_start, own_count, 0)
    places = (own_lengths[None, :] + jnp.arange(steps, dtype=jnp.int32)[:, None]).reshape(group)
    heads_here = w_query.shape[1] // HDIM

    def project(weight):
        return jnp.dot(attn_in, weight, preferred_element_type=jnp.float32).reshape(
            group, heads_here, HDIM
        )

    query_part = rotate(project(w_query), places).astype(jnp.bfloat16)
    key_part = rotate(project(w_key), places).astype(jnp.bfloat16)
    value_part = project(w_value).astype(jnp.bfloat16)
    every = lax.all_gather(
        jnp.stack([query_part, key_part, value_part], axis=0), "seq", axis=0, tiled=False
    )
    head_count = n_seq * heads_here
    every = jnp.moveaxis(every, 0, 2).reshape(3, steps, own_count, head_count, HDIM)
    queries = every[0]

    span = k_cache.shape[1]
    first_place = seq_index * span
    places_here = first_place + jnp.arange(span, dtype=jnp.int32)
    own_empty = lax.dynamic_slice_in_dim(empty_blocks, own_start, own_count, 0)
    local_blocks = lax.dynamic_slice_in_dim(own_empty, first_place // BLK, span // BLK, 1)
    blocked = jnp.broadcast_to(local_blocks[:, :, None], (own_count, span // BLK, BLK)).reshape(
        own_count, span
    )
    live_mask = ((places_here[None, :] < own_lengths[:, None]) & (blocked == 0))[None, :, None, :]
    cache_keys = k_cache.reshape(own_count, span, head_count, HDIM)
    cache_values = v_cache.reshape(own_count, span, head_count, HDIM)
    score_scale = 1.0 / math.sqrt(HDIM)
    cached = (
        jnp.einsum("trhd,rphd->trhp", queries, cache_keys, preferred_element_type=jnp.float32)
        * score_scale
    )
    local_top = jnp.max(jnp.where(live_mask, cached, negative), axis=3)
    local_weights = jnp.where(live_mask, jnp.exp(cached - local_top[..., None]), 0.0)
    local_totals = jnp.sum(local_weights, axis=3)
    local_mixture = jnp.einsum(
        "trhp,rphd->trhd",
        local_weights.astype(jnp.bfloat16),
        cache_values,
        preferred_element_type=jnp.float32,
    )

    def by_owner(values):
        rest = values.shape[3:]
        split = values.reshape((steps, own_count, n_seq, heads_here) + rest)
        return jnp.moveaxis(split, 2, 0).reshape(n_seq, -1)

    mix_len = group * heads_here * HDIM
    stat_len = group * heads_here
    packed = jnp.concatenate(
        [by_owner(local_mixture), by_owner(local_top), by_owner(local_totals)], axis=1
    )
    got = lax.all_to_all(packed, "seq", 0, 0, tiled=True)
    got_mixture = got[:, :mix_len].reshape(n_seq, steps, own_count, heads_here, HDIM)
    got_top = got[:, mix_len : mix_len + stat_len].reshape(n_seq, steps, own_count, heads_here)
    got_totals = got[:, mix_len + stat_len :].reshape(n_seq, steps, own_count, heads_here)

    own_queries = query_part.reshape(steps, own_count, heads_here, HDIM)
    own_keys = key_part.reshape(steps, own_count, heads_here, HDIM)
    own_values = value_part.reshape(steps, own_count, heads_here, HDIM)
    fresh_scores = (
        jnp.einsum("trhd,urhd->trhu", own_queries, own_keys, preferred_element_type=jnp.float32)
        * score_scale
    )
    causal = (jnp.arange(steps)[None, :] <= jnp.arange(steps)[:, None])[:, None, None, :]
    fresh_top = jnp.max(jnp.where(causal, fresh_scores, negative), axis=3)
    fresh_weights = jnp.where(causal, jnp.exp(fresh_scores - fresh_top[..., None]), 0.0)
    fresh_mixture = jnp.einsum(
        "trhu,urhd->trhd",
        fresh_weights.astype(jnp.bfloat16),
        own_values,
        preferred_element_type=jnp.float32,
    )
    top_score = jnp.maximum(jnp.max(got_top, axis=0), fresh_top)
    cache_factor = jnp.exp(got_top - top_score[None])
    fresh_factor = jnp.exp(fresh_top - top_score)
    totals = jnp.sum(got_totals * cache_factor, axis=0) + jnp.sum(fresh_weights, axis=3) * fresh_factor
    mixture = (
        jnp.sum(got_mixture * cache_factor[..., None], axis=0)
        + fresh_mixture * fresh_factor[..., None]
    )
    own_heads = (mixture / totals[..., None]).astype(jnp.bfloat16).reshape(
        group, heads_here * HDIM
    )

    attn_part = jnp.dot(own_heads, w_out, preferred_element_type=jnp.float32)
    attn_parts = lax.all_gather(attn_part.astype(jnp.bfloat16), "seq", axis=0, tiled=False)
    resid_group = embedded + jnp.sum(attn_parts.astype(jnp.float32), axis=0)
    resid_share = lax.dynamic_slice_in_dim(resid_group, seq_index * share, share, 0)
    moe_group = rms_scale(resid_group, moe_gain).astype(jnp.bfloat16)
    rounds = n_exp.bit_length() - 1
    if n_exp == 1 << rounds:
        flipped = jnp.arange(n_exp, dtype=jnp.int32) ^ lax.axis_index("exp")
        block = sum(((flipped >> bit) & 1) << (rounds - 1 - bit) for bit in range(rounds))
        for level in reversed(range(rounds)):
            partner = [(i, i ^ (1 << level)) for i in range(n_exp)]
            moe_group = jnp.concatenate([moe_group, lax.ppermute(moe_group, "exp", partner)], 0)
        moe_in = jnp.take(moe_group.reshape(n_exp, group, width), block, axis=0).reshape(
            tokens, width
        )
    else:
        moe_in = lax.all_gather(moe_group, "exp", axis=0, tiled=True)

    router = jax.nn.sigmoid(jnp.dot(moe_in, w_router, preferred_element_type=jnp.float32))
    expert_count = w_router.shape[1]
    chosen_ids = grouped(expert_ids)
    picked = chosen_ids[:, :, None] == jnp.arange(expert_count, dtype=jnp.int32)[None, None, :]
    chosen = jnp.sum(jnp.where(picked, router[:, None, :], 0.0), axis=2)
    gate_weights = chosen / jnp.sum(chosen, axis=1, keepdims=True)
    rows_here = gate_pieces.shape[0]
    row_expert = (owner_index * rows_here + jnp.arange(rows_here, dtype=jnp.int32)) // PIECES
    token_weight = jnp.sum(
        jnp.where(
            chosen_ids[:, :, None] == row_expert[None, None, :], gate_weights[:, :, None], 0.0
        ),
        axis=1,
    )
    share_count = tokens // n_seq
    share_start = seq_index * share_count
    token_place = jnp.arange(tokens, dtype=jnp.int32)
    shared_mask = (
        (token_place >= share_start) & (token_place < share_start + share_count)
    ).astype(jnp.float32)[:, None]
    lanes = -(-(rows_here + 1) // 128) * 128
    weight_table = jnp.pad(
        jnp.concatenate([token_weight, shared_mask], axis=1), ((0, 0), (0, lanes - rows_here - 1))
    )
    term_rows = experts(
        moe_in, weight_table, gate_pieces, up_pieces, down_pieces,
        shared_gate, shared_up, shared_down,
    )

    term_sum = jnp.sum(
        lax.all_to_all(
            term_rows.reshape(n_dev, share, width),
            ("exp", "seq"),
            0,
            0,
            tiled=True,
        ).astype(jnp.float32),
        axis=0,
    )
    final_share = resid_share + term_sum
    norms_share = jnp.sqrt(jnp.mean(final_share * final_share, axis=-1))
    head_share = rms_scale(final_share, final_gain).astype(jnp.bfloat16)
    if n_exp == 1 << rounds:
        head_in = lax.all_gather(head_share, "seq", axis=0, tiled=True)
        for level in reversed(range(rounds)):
            partner = [(i, i ^ (1 << level)) for i in range(n_exp)]
            head_in = jnp.concatenate([head_in, lax.ppermute(head_in, "exp", partner)], 0)
        local_best = jnp.max(jnp.dot(head_in, w_head, preferred_element_type=jnp.float32), axis=-1)
        local_best = jnp.take(local_best.reshape(n_exp, n_seq, share), block, axis=0)
        local_best = jnp.swapaxes(local_best, 0, 1).reshape(tokens)
    else:
        head_in = gather_all(head_share).reshape(tokens, width)
        local_best = jnp.max(jnp.dot(head_in, w_head, preferred_element_type=jnp.float32), axis=-1)
    message = jnp.concatenate([local_best, norms_share], axis=0)
    heard = lax.all_to_all(
        jnp.broadcast_to(message[None, :], (n_dev, message.shape[0])),
        ("seq", "exp"),
        0,
        0,
        tiled=True,
    )
    greatest_logits = natural(jnp.max(heard[:, :tokens], axis=0))
    hidden_norms = natural(heard[:, tokens:].reshape(tokens))
    return (hidden_norms, greatest_logits)


def solution(mesh):
    in_specs = (
        P(),
        P(),
        P(),
        P(),
        P(("seq", "exp"), None),
        P(),
        P(None, "seq"),
        P(None, "seq"),
        P(None, "seq"),
        P("seq", None),
        P("exp", "seq", None),
        P("exp", "seq", None),
        P(),
        P(),
        P(("seq", "exp"), None, None),
        P(("seq", "exp"), None, None),
        P(("seq", "exp"), None, None),
        P(None, "exp"),
        P(None, "exp"),
        P("exp", None),
        P(),
        P(None, ("seq", "exp")),
    )
    out_specs = (P(), P())
    return jax.shard_map(
        on_device, mesh=mesh, in_specs=in_specs, out_specs=out_specs, check_vma=False
    )
```
